256 devices in a mesh: con: 4 (over z_hi), grid: 64 (over z_lo, y, x, core).
Axes of the slice: x: 4, y: 4, z: 8 (z_hi: 4, z_lo: 2; z = z_hi * 2 + z_lo), core: 2. Of those that a mesh axis runs over, the one named last changes fastest.
Arguments:
- velocity: bfloat16 [8, 2, 4096, 4096], P('con', None, 'grid'), may hold values from -6 to 6
- seed_adjoint: bfloat16 [8, 2, 4096, 4096], P('con', None, 'grid'), may hold values from -6 to 6
- land_mask: int32 [4096, 4096], P('grid'), may hold values from 0 to 2
- inv_x: bfloat16 [32, 128, 128], replicated, may hold values from -0.5 to 0.5
- inv_y: bfloat16 [32, 128, 128], replicated, may hold values from -0.5 to 0.5
- weights: float32 [8], P('con'), may hold values from 0.05 to 0.5
Outputs:
- velocity_adjoint: float32 [8, 2, 4096, 4096], P('con', None, 'grid')
The draws below stay inside these ranges and needn't reach their ends.
Inputs may be any that keep to these rules, and one draw needn't show every extreme that they name: `land_mask`: 0 marks land, 1 a wet interior cell, 2 an open-boundary cell whose value is prescribed.
All inputs are finite; a program needn't handle non-finite values.
Results may differ from the reference program's by a relative error of at most 0.0039.
Values may be sent and summed in bfloat16 or wider, within the bound.
No kernel may reach another device: no remote copies, remote signals or barrier semaphores. Data moves between devices by JAX's collectives and lax.ppermute only.
A program may use at most 64 MiB of HBM per device.

```python
import math
import jax
import jax.numpy as jnp
from jax import lax

C = 8
BLK = 128
SIDE = 4096
NBLK = 32


def with_ends(entries, own_key, low, top_value):
    longest = entries.shape.index(max(entries.shape))
    spots = []
    for shift in (0, 1):
        where = [jax.random.randint(jax.random.fold_in(own_key, axis), (), 0, length) for axis, length in enumerate(entries.shape)]
        where[longest] = (where[longest] + shift) % entries.shape[longest]
        spots.append(tuple(where))
    return entries.at[spots[0]].set(low).at[spots[1]].set(top_value)


def block_scale(stream_key, extent, shards, least, high):
    level = 1.0
    for dim, shards_of in shards:
        steps = jax.random.uniform(jax.random.fold_in(jax.random.fold_in(stream_key, 6), dim), (shards_of,), jnp.float32, least / len(shards), high / len(shards))
        level = level * jnp.repeat(jnp.exp(steps), extent[dim] // shards_of).reshape((-1,) + (1,) * (len(extent) - 1 - dim))
    return level


def noise(rng, dims, scale, reach, split=(), held_as=jnp.bfloat16):
    array = scale * jax.random.normal(rng, dims, jnp.float32)
    if split:
        array = array * block_scale(rng, dims, split, -0.22, 0.18)
    return jnp.clip(array, -reach, reach).astype(held_as)


def setup_inputs(seed: int = 0) -> dict:
    key_of = jax.random.split(jax.random.key(seed), 7)
    velocity = noise(key_of[0], (C, 2, SIDE, SIDE), 1.0, 6.0, ((0, 4), (2, 64)))
    seed_adjoint = noise(key_of[1], (C, 2, SIDE, SIDE), 1.0, 6.0, ((0, 4), (2, 64)))
    land_mask = with_ends(jax.random.randint(key_of[2], (SIDE, SIDE), 0, 3), jax.random.fold_in(key_of[2], 1), 0, 2).astype(jnp.int32)
    inv_x = noise(key_of[3], (NBLK, BLK, BLK), BLK ** -0.5, 0.5)
    inv_y = noise(key_of[4], (NBLK, BLK, BLK), BLK ** -0.5, 0.5)
    weights = jnp.clip(jnp.exp(math.log(0.5) - 2.3025851 * jax.random.uniform(key_of[5], (C,), jnp.float32) ** block_scale(key_of[5], (C,), ((0, 4),), -0.2, 0.2)), 0.05, 0.5)
    return dict(velocity=velocity, seed_adjoint=seed_adjoint, land_mask=land_mask, inv_x=inv_x, inv_y=inv_y, weights=weights)


def solve_blocks(field, inverse):
    shape = field.shape
    blocks = field.astype(jnp.float32).reshape(shape[:-1] + (NBLK, BLK))
    result = jnp.einsum('pyki,kji->pykj', blocks, inverse.astype(jnp.float32))
    return result.reshape(shape)

def reference(velocity, seed_adjoint, land_mask, inv_x, inv_y, weights):
    sea = (land_mask == 1).astype(jnp.float32)
    sea_half = sea.astype(jnp.bfloat16)
    squares = jnp.zeros((SIDE, SIDE), jnp.float32)
    for con_index in range(C):
        vel = velocity[con_index].astype(jnp.float32)
        squares = squares + weights[con_index] * lax.optimization_barrier(jnp.sum(vel * vel, axis=0))
    speed = jnp.sqrt(0.25 + squares)
    inner = jnp.zeros((SIDE, SIDE), jnp.float32)
    solved = []
    for con_index in range(C):
        across = solve_blocks(seed_adjoint[con_index], inv_x).astype(jnp.bfloat16)
        masked = jnp.swapaxes(across, 1, 2) * sea_half[None]
        rows = solve_blocks(masked, inv_y)
        solved.append(rows)
        inner = inner + lax.optimization_barrier(jnp.sum(rows * velocity[con_index].astype(jnp.float32), axis=0))
    results = []
    for con_index in range(C):
        vel = velocity[con_index].astype(jnp.float32)
        term = -0.5 * sea * speed * solved[con_index] - 0.5 * sea * weights[con_index] * vel * inner / speed
        results.append(term)
    return jnp.stack(results, axis=0)
```

```python
import jax
import jax.numpy as jnp
from jax import lax
from jax.sharding import PartitionSpec as P

BLK = 128


def con_sum(part, link_type):
    count = lax.axis_size("con")
    me = lax.axis_index("con")
    rows = part.shape[0]
    quarters = part.reshape((count, rows // count) + part.shape[1:])
    total = lax.dynamic_index_in_dim(quarters, me, 0, keepdims=False).astype(jnp.float32)
    for shift in range(1, count):
        pairs = [(i, (i + shift) % count) for i in range(count)]
        piece = lax.dynamic_index_in_dim(quarters, (me + shift) % count, 0, keepdims=False)
        total = total + lax.ppermute(piece.astype(link_type), "con", pairs).astype(jnp.float32)
    mine = total.astype(link_type)
    pieces = [mine]
    for shift in range(1, count):
        pairs = [(i, (i + shift) % count) for i in range(count)]
        pieces.append(lax.ppermute(mine, "con", pairs))
    ordered = jnp.stack([pieces[(-t) % count] for t in range(count)])
    gathered = jnp.roll(ordered, me, axis=0)
    return gathered.reshape(part.shape).astype(jnp.float32)


def local(velocity, seed_adjoint, land_mask, inv_x, inv_y, weights):
    nblocks = inv_x.shape[0]
    con_local = velocity.shape[0]
    cols_local = seed_adjoint.shape[2]
    full_side = seed_adjoint.shape[3]
    rows_local = velocity.shape[2]
    vel_float = velocity.astype(jnp.float32)
    weight_full = weights[:, None, None, None]
    local_squares = jnp.sum(weight_full * vel_float * vel_float, axis=(0, 1))
    local_squares, seed_adjoint = lax.optimization_barrier((local_squares, seed_adjoint))
    squares = con_sum(local_squares, jnp.float32)
    sea_bool = land_mask == 1
    sea_float = sea_bool.astype(jnp.float32)
    sea_turned = jnp.swapaxes(sea_bool, 0, 1).astype(jnp.bfloat16)
    blocks_x = seed_adjoint.reshape(con_local, 2, cols_local, nblocks, BLK)
    across = jnp.einsum("cpyki,kji->cpykj", blocks_x, inv_x, preferred_element_type=jnp.float32)
    across = across.astype(jnp.bfloat16).reshape(con_local, 2, cols_local, full_side)
    arrived = lax.all_to_all(across, "grid", split_axis=3, concat_axis=2, tiled=True)
    count = arrived.shape[0]
    masked = arrived * sea_turned[None, None]
    blocks_y = masked.reshape(count, 2, nblocks, BLK, rows_local)
    solved = jnp.einsum("cpkiu,kji->cpukj", blocks_y, inv_y, preferred_element_type=jnp.float32)
    rhs_adjoint = solved.reshape(count, 2, rows_local, nblocks * BLK)
    local_inner = jnp.sum(rhs_adjoint * vel_float, axis=(0, 1))
    inner = con_sum(local_inner, jnp.bfloat16)
    speed = jnp.sqrt(0.25 + squares)
    first = -0.5 * sea_float * speed * rhs_adjoint
    second = -0.5 * sea_float * weight_full * vel_float * inner / speed
    return first + second


def solution(mesh):
    return jax.shard_map(
        local,
        mesh=mesh,
        in_specs=(
            P("con", None, "grid", None),
            P("con", None, "grid", None),
            P("grid", None),
            P(),
            P(),
            P("con"),
        ),
        out_specs=P("con", None, "grid", None),
        check_vma=False,
    )
```

```python
import jax
import jax.numpy as jnp
from jax import lax
from jax.sharding import PartitionSpec as P

BLK = 128


def con_sum(part, link_type):
    count = lax.axis_size("con")
    me = lax.axis_index("con")
    rows = part.shape[0]
    quarters = part.reshape((count, rows // count) + part.shape[1:])
    total = lax.dynamic_index_in_dim(quarters, me, 0, keepdims=False).astype(jnp.float32)
    for shift in range(1, count):
        pairs = [(i, (i + shift) % count) for i in range(count)]
        piece = lax.dynamic_index_in_dim(quarters, (me + shift) % count, 0, keepdims=False)
        total = total + lax.ppermute(piece.astype(link_type), "con", pairs).astype(jnp.float32)
    mine = total.astype(link_type)
    pieces = [mine]
    for shift in range(1, count):
        pairs = [(i, (i + shift) % count) for i in range(count)]
        pieces.append(lax.ppermute(mine, "con", pairs))
    ordered = jnp.stack([pieces[(-t) % count] for t in range(count)])
    gathered = jnp.roll(ordered, me, axis=0)
    return gathered.reshape(part.shape).astype(jnp.float32)


def local(velocity, seed_adjoint, land_mask, inv_x, inv_y, weights):
    nblocks = inv_x.shape[0]
    con_local = velocity.shape[0]
    cols_local = seed_adjoint.shape[2]
    full_side = seed_adjoint.shape[3]
    rows_local = velocity.shape[2]
    vel_float = velocity.astype(jnp.float32)
    weight_full = weights[:, None, None, None]
    local_squares = jnp.sum(weight_full * vel_float * vel_float, axis=(0, 1))
    sea_bool = land_mask == 1
    sea_float = sea_bool.astype(jnp.float32)
    sea_turned = jnp.swapaxes(sea_bool, 0, 1).astype(jnp.bfloat16)
    blocks_x = seed_adjoint.reshape(con_local, 2, cols_local, nblocks, BLK)
    across = jnp.einsum("cpyki,kji->cpykj", blocks_x, inv_x, preferred_element_type=jnp.float32)
    across = across.astype(jnp.bfloat16).reshape(con_local, 2, cols_local, full_side)
    across, local_squares = lax.optimization_barrier((across, local_squares))
    squares = con_sum(local_squares, jnp.bfloat16)
    arrived = lax.all_to_all(across, "grid", split_axis=3, concat_axis=2, tiled=True)
    count = arrived.shape[0]
    masked = arrived * sea_turned[None, None]
    blocks_y = masked.reshape(count, 2, nblocks, BLK, rows_local)
    solved = jnp.einsum("cpkiu,kji->cpukj", blocks_y, inv_y, preferred_element_type=jnp.float32)
    rhs_adjoint = solved.reshape(count, 2, rows_local, nblocks * BLK)
    local_inner = jnp.sum(rhs_adjoint * vel_float, axis=(0, 1))
    inner = con_sum(local_inner, jnp.bfloat16)
    speed = jnp.sqrt(0.25 + squares)
    first = -0.5 * sea_float * speed * rhs_adjoint
    second = -0.5 * sea_float * weight_full * vel_float * inner / speed
    return first + second


def solution(mesh):
    return jax.shard_map(
        local,
        mesh=mesh,
        in_specs=(
            P("con", None, "grid", None),
            P("con", None, "grid", None),
            P("grid", None),
            P(),
            P(),
            P("con"),
        ),
        out_specs=P("con", None, "grid", None),
        check_vma=False,
    )
```

```python
import jax
import jax.numpy as jnp
from jax import lax
from jax.experimental import pallas as pl
from jax.experimental.pallas import tpu as pltpu
from jax.sharding import PartitionSpec as P

BLK = 128
GROUP = 4
INTERPRET = False


def con_sum(part, link_type):
    count = lax.axis_size("con")
    me = lax.axis_index("con")
    rows = part.shape[0]
    quarters = part.reshape((count, rows // count) + part.shape[1:])
    total = lax.dynamic_index_in_dim(quarters, me, 0, keepdims=False).astype(jnp.float32)
    for shift in range(1, count):
        pairs = [(i, (i + shift) % count) for i in range(count)]
        piece = lax.dynamic_index_in_dim(quarters, (me + shift) % count, 0, keepdims=False)
        total = total + lax.ppermute(piece.astype(link_type), "con", pairs).astype(jnp.float32)
    mine = total.astype(link_type)
    pieces = [mine]
    for shift in range(1, count):
        pairs = [(i, (i + shift) % count) for i in range(count)]
        pieces.append(lax.ppermute(mine, "con", pairs))
    ordered = jnp.stack([pieces[(-t) % count] for t in range(count)])
    gathered = jnp.roll(ordered, me, axis=0)
    return gathered.reshape(part.shape).astype(jnp.float32)


def x_solve_kernel(s_ref, w_ref, o_ref):
    for b in range(w_ref.shape[0]):
        block = s_ref[:, b * BLK:(b + 1) * BLK]
        out = lax.dot_general(w_ref[b], block, (((1,), (1,)), ((), ())), preferred_element_type=jnp.float32)
        o_ref[b * BLK:(b + 1) * BLK, :] = out.astype(o_ref.dtype)


def x_solve(rows, inv_x):
    lanes, side = rows.shape
    nblocks = inv_x.shape[0]
    return pl.pallas_call(
        x_solve_kernel,
        grid=(nblocks // GROUP,),
        in_specs=[
            pl.BlockSpec((lanes, GROUP * BLK), lambda g: (0, g)),
            pl.BlockSpec((GROUP, BLK, BLK), lambda g: (g, 0, 0)),
        ],
        out_specs=pl.BlockSpec((GROUP * BLK, lanes), lambda g: (g, 0)),
        out_shape=jax.ShapeDtypeStruct((side, lanes), jnp.bfloat16),
        interpret=INTERPRET,
    )(rows, inv_x)


def y_solve_kernel(r_ref, m_ref, w_ref, v_ref, g_ref, i_ref):
    half = r_ref.shape[0] // (2 * w_ref.shape[0])
    count = v_ref.shape[0]
    lane = lax.broadcasted_iota(jnp.int32, (half, BLK), 1)
    low = lane < half
    for b in range(w_ref.shape[0]):
        cols = slice(b * BLK, (b + 1) * BLK)
        sea = m_ref[:, cols] == 1
        weight = w_ref[b]
        total = jnp.zeros((half, BLK), jnp.float32)
        for q in range(count):
            tile = slice((q // 2) * BLK, (q // 2 + 1) * BLK)
            first = r_ref[2 * b * half:(2 * b + 1) * half, tile].astype(jnp.float32)
            second = r_ref[(2 * b + 1) * half:(2 * b + 2) * half, tile].astype(jnp.float32)
            if q % 2 == 0:
                joined = jnp.where(low, first, pltpu.roll(second, half, 1))
            else:
                joined = jnp.where(low, pltpu.roll(first, half, 1), second)
            joined = jnp.where(sea, joined, 0.0).astype(jnp.bfloat16)
            out = lax.dot_general(joined, weight, (((1,), (1,)), ((), ())), preferred_element_type=jnp.float32)
            g_ref[q, :, cols] = out
            total = total + out * v_ref[q, :, cols].astype(jnp.float32)
        i_ref[:, cols] = total


def y_solve(arrived, land_mask, inv_y, vel):
    count, rows_local, side = vel.shape
    nblocks = inv_y.shape[0]
    return pl.pallas_call(
        y_solve_kernel,
        grid=(nblocks // GROUP,),
        in_specs=[
            pl.BlockSpec((GROUP * 2 * rows_local, arrived.shape[1]), lambda g: (g, 0)),
            pl.BlockSpec((rows_local, GROUP * BLK), lambda g: (0, g)),
            pl.BlockSpec((GROUP, BLK, BLK), lambda g: (g, 0, 0)),
            pl.BlockSpec((count, rows_local, GROUP * BLK), lambda g: (0, 0, g)),
        ],
        out_specs=[
            pl.BlockSpec((count, rows_local, GROUP * BLK), lambda g: (0, 0, g)),
            pl.BlockSpec((rows_local, GROUP * BLK), lambda g: (0, g)),
        ],
        out_shape=[
            jax.ShapeDtypeStruct((count, rows_local, side), jnp.float32),
            jax.ShapeDtypeStruct((rows_local, side), jnp.float32),
        ],
        interpret=INTERPRET,
    )(arrived, land_mask, inv_y, vel)


def local(velocity, seed_adjoint, land_mask, inv_x, inv_y, weights):
    con_local = velocity.shape[0]
    cols_local = seed_adjoint.shape[2]
    full_side = seed_adjoint.shape[3]
    rows_local = velocity.shape[2]
    vel_float = velocity.astype(jnp.float32)
    weight_full = weights[:, None, None, None]
    local_squares = jnp.sum(weight_full * vel_float * vel_float, axis=(0, 1))
    sea_float = (land_mask == 1).astype(jnp.float32)
    across = x_solve(seed_adjoint.reshape(con_local * 2 * cols_local, full_side), inv_x)
    across, local_squares = lax.optimization_barrier((across, local_squares))
    squares = con_sum(local_squares, jnp.bfloat16)
    arrived = lax.all_to_all(across, "grid", split_axis=0, concat_axis=0, tiled=True)
    solved, local_inner = y_solve(arrived, land_mask, inv_y, velocity.reshape(con_local * 2, rows_local, full_side))
    rhs_adjoint = solved.reshape(con_local, 2, rows_local, full_side)
    inner = con_sum(local_inner, jnp.bfloat16)
    speed = jnp.sqrt(0.25 + squares)
    first = -0.5 * sea_float * speed * rhs_adjoint
    second = -0.5 * sea_float * weight_full * vel_float * inner / speed
    return first + second


def solution(mesh):
    return jax.shard_map(
        local,
        mesh=mesh,
        in_specs=(
            P("con", None, "grid", None),
            P("con", None, "grid", None),
            P("grid", None),
            P(),
            P(),
            P("con"),
        ),
        out_specs=P("con", None, "grid", None),
        check_vma=False,
    )
```

```python
import jax
import jax.numpy as jnp
from jax import lax
from jax.experimental import pallas as pl
from jax.experimental.pallas import tpu as pltpu
from jax.sharding import PartitionSpec as P

BLK = 128
GROUP = 4
INTERPRET = False


def con_sum(part, link_type):
    count = lax.axis_size("con")
    rows = part.shape[0]
    quarters = part.astype(link_type).reshape((count, rows // count) + part.shape[1:])
    arrived = lax.all_to_all(quarters, "con", 0, 0, tiled=True)
    mine = jnp.sum(arrived.astype(jnp.float32), axis=0).astype(link_type)
    spread = jnp.broadcast_to(mine[None], (count,) + mine.shape)
    gathered = lax.all_to_all(spread, "con", 0, 0, tiled=True)
    return gathered.reshape(part.shape).astype(jnp.float32)


def x_solve_kernel(s_ref, w_ref, o_ref):
    for b in range(w_ref.shape[0]):
        block = s_ref[:, b * BLK:(b + 1) * BLK]
        out = lax.dot_general(w_ref[b], block, (((1,), (1,)), ((), ())), preferred_element_type=jnp.float32)
        o_ref[b * BLK:(b + 1) * BLK, :] = out.astype(o_ref.dtype)


def x_solve(rows, inv_x):
    lanes, side = rows.shape
    nblocks = inv_x.shape[0]
    return pl.pallas_call(
        x_solve_kernel,
        grid=(nblocks // GROUP,),
        in_specs=[
            pl.BlockSpec((lanes, GROUP * BLK), lambda g: (0, g)),
            pl.BlockSpec((GROUP, BLK, BLK), lambda g: (g, 0, 0)),
        ],
        out_specs=pl.BlockSpec((GROUP * BLK, lanes), lambda g: (g, 0)),
        out_shape=jax.ShapeDtypeStruct((side, lanes), jnp.bfloat16),
        interpret=INTERPRET,
    )(rows, inv_x)


def y_solve_kernel(r_ref, m_ref, w_ref, v_ref, g_ref, i_ref):
    half = r_ref.shape[0] // (2 * w_ref.shape[0])
    count = v_ref.shape[0]
    lane = lax.broadcasted_iota(jnp.int32, (half, BLK), 1)
    low = lane < half
    for b in range(w_ref.shape[0]):
        cols = slice(b * BLK, (b + 1) * BLK)
        sea = m_ref[:, cols] == 1
        weight = w_ref[b]
        total = jnp.zeros((half, BLK), jnp.float32)
        for q in range(count):
            tile = slice((q // 2) * BLK, (q // 2 + 1) * BLK)
            first = r_ref[2 * b * half:(2 * b + 1) * half, tile].astype(jnp.float32)
            second = r_ref[(2 * b + 1) * half:(2 * b + 2) * half, tile].astype(jnp.float32)
            if q % 2 == 0:
                joined = jnp.where(low, first, pltpu.roll(second, half, 1))
            else:
                joined = jnp.where(low, pltpu.roll(first, half, 1), second)
            joined = jnp.where(sea, joined, 0.0).astype(jnp.bfloat16)
            out = lax.dot_general(joined, weight, (((1,), (1,)), ((), ())), preferred_element_type=jnp.float32)
            g_ref[q, :, cols] = out
            total = total + out * v_ref[q, :, cols].astype(jnp.float32)
        i_ref[:, cols] = total


def y_solve(arrived, land_mask, inv_y, vel):
    count, rows_local, side = vel.shape
    nblocks = inv_y.shape[0]
    return pl.pallas_call(
        y_solve_kernel,
        grid=(nblocks // GROUP,),
        in_specs=[
            pl.BlockSpec((GROUP * 2 * rows_local, arrived.shape[1]), lambda g: (g, 0)),
            pl.BlockSpec((rows_local, GROUP * BLK), lambda g: (0, g)),
            pl.BlockSpec((GROUP, BLK, BLK), lambda g: (g, 0, 0)),
            pl.BlockSpec((count, rows_local, GROUP * BLK), lambda g: (0, 0, g)),
        ],
        out_specs=[
            pl.BlockSpec((count, rows_local, GROUP * BLK), lambda g: (0, 0, g)),
            pl.BlockSpec((rows_local, GROUP * BLK), lambda g: (0, g)),
        ],
        out_shape=[
            jax.ShapeDtypeStruct((count, rows_local, side), jnp.float32),
            jax.ShapeDtypeStruct((rows_local, side), jnp.float32),
        ],
        interpret=INTERPRET,
    )(arrived, land_mask, inv_y, vel)


def local(velocity, seed_adjoint, land_mask, inv_x, inv_y, weights):
    con_local = velocity.shape[0]
    cols_local = seed_adjoint.shape[2]
    full_side = seed_adjoint.shape[3]
    rows_local = velocity.shape[2]
    vel_float = velocity.astype(jnp.float32)
    weight_full = weights[:, None, None, None]
    local_squares = jnp.sum(weight_full * vel_float * vel_float, axis=(0, 1))
    sea_float = (land_mask == 1).astype(jnp.float32)
    across = x_solve(seed_adjoint.reshape(con_local * 2 * cols_local, full_side), inv_x)
    across, local_squares = lax.optimization_barrier((across, local_squares))
    squares = con_sum(local_squares, jnp.bfloat16)
    arrived = lax.all_to_all(across, "grid", split_axis=0, concat_axis=0, tiled=True)
    solved, local_inner = y_solve(arrived, land_mask, inv_y, velocity.reshape(con_local * 2, rows_local, full_side))
    rhs_adjoint = solved.reshape(con_local, 2, rows_local, full_side)
    inner = con_sum(local_inner, jnp.bfloat16)
    speed = jnp.sqrt(0.25 + squares)
    first = -0.5 * sea_float * speed * rhs_adjoint
    second = -0.5 * sea_float * weight_full * vel_float * inner / speed
    return first + second


def solution(mesh):
    return jax.shard_map(
        local,
        mesh=mesh,
        in_specs=(
            P("con", None, "grid", None),
            P("con", None, "grid", None),
            P("grid", None),
            P(),
            P(),
            P("con"),
        ),
        out_specs=P("con", None, "grid", None),
        check_vma=False,
    )
```

```python
import jax
import jax.numpy as jnp
from jax import lax
from jax.experimental import pallas as pl
from jax.experimental.pallas import tpu as pltpu
from jax.sharding import PartitionSpec as P

BLK = 128
GROUP = 4
INTERPRET = False


def con_sum(part, link_type):
    count = lax.axis_size("con")
    me = lax.axis_index("con")
    rows = part.shape[0]
    quarters = part.reshape((count, rows // count) + part.shape[1:])
    total = lax.dynamic_index_in_dim(quarters, me, 0, keepdims=False).astype(jnp.float32)
    for shift in range(1, count):
        pairs = [(i, (i + shift) % count) for i in range(count)]
        piece = lax.dynamic_index_in_dim(quarters, (me + shift) % count, 0, keepdims=False)
        total = total + lax.ppermute(piece.astype(link_type), "con", pairs).astype(jnp.float32)
    mine = total.astype(link_type)
    pieces = [mine]
    for shift in range(1, count):
        pairs = [(i, (i + shift) % count) for i in range(count)]
        pieces.append(lax.ppermute(mine, "con", pairs))
    ordered = jnp.stack([pieces[(-t) % count] for t in range(count)])
    gathered = jnp.roll(ordered, me, axis=0)
    return gathered.reshape(part.shape).astype(jnp.float32)


def x_solve_kernel(s_ref, w_ref, o_ref):
    for b in range(w_ref.shape[0]):
        block = s_ref[:, b * BLK:(b + 1) * BLK]
        out = lax.dot_general(w_ref[b], block, (((1,), (1,)), ((), ())), preferred_element_type=jnp.float32)
        o_ref[b * BLK:(b + 1) * BLK, :] = out.astype(o_ref.dtype)


def x_solve(rows, inv_x):
    lanes, side = rows.shape
    nblocks = inv_x.shape[0]
    return pl.pallas_call(
        x_solve_kernel,
        grid=(nblocks // GROUP,),
        in_specs=[
            pl.BlockSpec((lanes, GROUP * BLK), lambda g: (0, g)),
            pl.BlockSpec((GROUP, BLK, BLK), lambda g: (g, 0, 0)),
        ],
        out_specs=pl.BlockSpec((GROUP * BLK, lanes), lambda g: (g, 0)),
        out_shape=jax.ShapeDtypeStruct((side, lanes), jnp.bfloat16),
        interpret=INTERPRET,
    )(rows, inv_x)


def y_solve_kernel(r_ref, m_ref, w_ref, v_ref, g_ref, i_ref):
    half = r_ref.shape[0] // (2 * w_ref.shape[0])
    count = v_ref.shape[0]
    lane = lax.broadcasted_iota(jnp.int32, (half, BLK), 1)
    low = lane < half
    for b in range(w_ref.shape[0]):
        cols = slice(b * BLK, (b + 1) * BLK)
        sea = m_ref[:, cols] == 1
        weight = w_ref[b]
        total = jnp.zeros((half, BLK), jnp.float32)
        for q in range(count):
            tile = slice((q // 2) * BLK, (q // 2 + 1) * BLK)
            first = r_ref[2 * b * half:(2 * b + 1) * half, tile].astype(jnp.float32)
            second = r_ref[(2 * b + 1) * half:(2 * b + 2) * half, tile].astype(jnp.float32)
            if q % 2 == 0:
                joined = jnp.where(low, first, pltpu.roll(second, half, 1))
            else:
                joined = jnp.where(low, pltpu.roll(first, half, 1), second)
            joined = jnp.where(sea, joined, 0.0).astype(jnp.bfloat16)
            out = lax.dot_general(joined, weight, (((1,), (1,)), ((), ())), preferred_element_type=jnp.float32)
            g_ref[q, :, cols] = out
            total = total + out * v_ref[q, :, cols].astype(jnp.float32)
        i_ref[:, cols] = total


def y_solve(arrived, land_mask, inv_y, vel):
    count, rows_local, side = vel.shape
    nblocks = inv_y.shape[0]
    return pl.pallas_call(
        y_solve_kernel,
        grid=(nblocks // GROUP,),
        in_specs=[
            pl.BlockSpec((GROUP * 2 * rows_local, arrived.shape[1]), lambda g: (g, 0)),
            pl.BlockSpec((rows_local, GROUP * BLK), lambda g: (0, g)),
            pl.BlockSpec((GROUP, BLK, BLK), lambda g: (g, 0, 0)),
            pl.BlockSpec((count, rows_local, GROUP * BLK), lambda g: (0, 0, g)),
        ],
        out_specs=[
            pl.BlockSpec((count, rows_local, GROUP * BLK), lambda g: (0, 0, g)),
            pl.BlockSpec((rows_local, GROUP * BLK), lambda g: (0, g)),
        ],
        out_shape=[
            jax.ShapeDtypeStruct((count, rows_local, side), jnp.float32),
            jax.ShapeDtypeStruct((rows_local, side), jnp.float32),
        ],
        interpret=INTERPRET,
    )(arrived, land_mask, inv_y, vel)


def local(velocity, seed_adjoint, land_mask, inv_x, inv_y, weights):
    con_local = velocity.shape[0]
    cols_local = seed_adjoint.shape[2]
    full_side = seed_adjoint.shape[3]
    rows_local = velocity.shape[2]
    vel_float = velocity.astype(jnp.float32)
    weight_full = weights[:, None, None, None]
    local_squares = jnp.sum(weight_full * vel_float * vel_float, axis=(0, 1))
    sea_float = (land_mask == 1).astype(jnp.float32)
    across = x_solve(seed_adjoint.reshape(con_local * 2 * cols_local, full_side), inv_x)
    arrived = lax.all_to_all(across, "grid", split_axis=0, concat_axis=0, tiled=True)
    solved, local_inner = y_solve(arrived, land_mask, inv_y, velocity.reshape(con_local * 2, rows_local, full_side))
    rhs_adjoint = solved.reshape(con_local, 2, rows_local, full_side)
    both = con_sum(jnp.concatenate([local_squares, local_inner], axis=0), jnp.bfloat16)
    squares, inner = both[:rows_local], both[rows_local:]
    speed = jnp.sqrt(0.25 + squares)
    first = -0.5 * sea_float * speed * rhs_adjoint
    second = -0.5 * sea_float * weight_full * vel_float * inner / speed
    return first + second


def solution(mesh):
    return jax.shard_map(
        local,
        mesh=mesh,
        in_specs=(
            P("con", None, "grid", None),
            P("con", None, "grid", None),
            P("grid", None),
            P(),
            P(),
            P("con"),
        ),
        out_specs=P("con", None, "grid", None),
        check_vma=False,
    )
```

```python
import jax
import jax.numpy as jnp
from jax import lax
from jax.experimental import pallas as pl
from jax.experimental.pallas import tpu as pltpu
from jax.sharding import PartitionSpec as P

BLK = 128
GROUP = 4
INTERPRET = False


def con_sum(part, link_type):
    count = lax.axis_size("con")
    me = lax.axis_index("con")
    rows = part.shape[0]
    quarters = part.reshape((count, rows // count) + part.shape[1:])
    total = lax.dynamic_index_in_dim(quarters, me, 0, keepdims=False).astype(jnp.float32)
    for shift in range(1, count):
        pairs = [(i, (i + shift) % count) for i in range(count)]
        piece = lax.dynamic_index_in_dim(quarters, (me + shift) % count, 0, keepdims=False)
        total = total + lax.ppermute(piece.astype(link_type), "con", pairs).astype(jnp.float32)
    mine = total.astype(link_type)
    pieces = [mine]
    for shift in range(1, count):
        pairs = [(i, (i + shift) % count) for i in range(count)]
        pieces.append(lax.ppermute(mine, "con", pairs))
    slots = []
    for q in range(count):
        source = (me - q) % count
        slot = pieces[0]
        for shift in range(1, count):
            slot = jnp.where(source == shift, pieces[shift], slot)
        slots.append(slot)
    return jnp.concatenate(slots, axis=0).astype(jnp.float32)


def x_solve_kernel(s_ref, w_ref, o_ref):
    for b in range(w_ref.shape[0]):
        block = s_ref[:, b * BLK:(b + 1) * BLK]
        out = lax.dot_general(w_ref[b], block, (((1,), (1,)), ((), ())), preferred_element_type=jnp.float32)
        o_ref[b * BLK:(b + 1) * BLK, :] = out.astype(o_ref.dtype)


def x_solve(rows, inv_x):
    lanes, side = rows.shape
    nblocks = inv_x.shape[0]
    return pl.pallas_call(
        x_solve_kernel,
        grid=(nblocks // GROUP,),
        in_specs=[
            pl.BlockSpec((lanes, GROUP * BLK), lambda g: (0, g)),
            pl.BlockSpec((GROUP, BLK, BLK), lambda g: (g, 0, 0)),
        ],
        out_specs=pl.BlockSpec((GROUP * BLK, lanes), lambda g: (g, 0)),
        out_shape=jax.ShapeDtypeStruct((side, lanes), jnp.bfloat16),
        interpret=INTERPRET,
    )(rows, inv_x)


def y_solve_kernel(r_ref, m_ref, w_ref, v_ref, g_ref, i_ref):
    half = r_ref.shape[0] // (2 * w_ref.shape[0])
    count = v_ref.shape[0]
    lane = lax.broadcasted_iota(jnp.int32, (half, BLK), 1)
    low = lane < half
    for b in range(w_ref.shape[0]):
        cols = slice(b * BLK, (b + 1) * BLK)
        sea = m_ref[:, cols] == 1
        weight = w_ref[b]
        total = jnp.zeros((half, BLK), jnp.float32)
        for q in range(count):
            tile = slice((q // 2) * BLK, (q // 2 + 1) * BLK)
            first = r_ref[2 * b * half:(2 * b + 1) * half, tile].astype(jnp.float32)
            second = r_ref[(2 * b + 1) * half:(2 * b + 2) * half, tile].astype(jnp.float32)
            if q % 2 == 0:
                joined = jnp.where(low, first, pltpu.roll(second, half, 1))
            else:
                joined = jnp.where(low, pltpu.roll(first, half, 1), second)
            joined = jnp.where(sea, joined, 0.0).astype(jnp.bfloat16)
            out = lax.dot_general(joined, weight, (((1,), (1,)), ((), ())), preferred_element_type=jnp.float32)
            g_ref[q, :, cols] = out
            total = total + out * v_ref[q, :, cols].astype(jnp.float32)
        i_ref[:, cols] = total


def y_solve(arrived, land_mask, inv_y, vel):
    count, rows_local, side = vel.shape
    nblocks = inv_y.shape[0]
    return pl.pallas_call(
        y_solve_kernel,
        grid=(nblocks // GROUP,),
        in_specs=[
            pl.BlockSpec((GROUP * 2 * rows_local, arrived.shape[1]), lambda g: (g, 0)),
            pl.BlockSpec((rows_local, GROUP * BLK), lambda g: (0, g)),
            pl.BlockSpec((GROUP, BLK, BLK), lambda g: (g, 0, 0)),
            pl.BlockSpec((count, rows_local, GROUP * BLK), lambda g: (0, 0, g)),
        ],
        out_specs=[
            pl.BlockSpec((count, rows_local, GROUP * BLK), lambda g: (0, 0, g)),
            pl.BlockSpec((rows_local, GROUP * BLK), lambda g: (0, g)),
        ],
        out_shape=[
            jax.ShapeDtypeStruct((count, rows_local, side), jnp.float32),
            jax.ShapeDtypeStruct((rows_local, side), jnp.float32),
        ],
        interpret=INTERPRET,
    )(arrived, land_mask, inv_y, vel)


def local(velocity, seed_adjoint, land_mask, inv_x, inv_y, weights):
    con_local = velocity.shape[0]
    cols_local = seed_adjoint.shape[2]
    full_side = seed_adjoint.shape[3]
    rows_local = velocity.shape[2]
    vel_float = velocity.astype(jnp.float32)
    weight_full = weights[:, None, None, None]
    local_squares = jnp.sum(weight_full * vel_float * vel_float, axis=(0, 1))
    sea_float = (land_mask == 1).astype(jnp.float32)
    across = x_solve(seed_adjoint.reshape(con_local * 2 * cols_local, full_side), inv_x)
    arrived = lax.all_to_all(across, "grid", split_axis=0, concat_axis=0, tiled=True)
    arrived, local_squares = lax.optimization_barrier((arrived, local_squares))
    squares = con_sum(local_squares, jnp.bfloat16)
    solved, local_inner = y_solve(arrived, land_mask, inv_y, velocity.reshape(con_local * 2, rows_local, full_side))
    rhs_adjoint = solved.reshape(con_local, 2, rows_local, full_side)
    inner = con_sum(local_inner, jnp.bfloat16)
    speed = jnp.sqrt(0.25 + squares)
    first = -0.5 * sea_float * speed * rhs_adjoint
    second = -0.5 * sea_float * weight_full * vel_float * inner / speed
    return first + second


def solution(mesh):
    return jax.shard_map(
        local,
        mesh=mesh,
        in_specs=(
            P("con", None, "grid", None),
            P("con", None, "grid", None),
            P("grid", None),
            P(),
            P(),
            P("con"),
        ),
        out_specs=P("con", None, "grid", None),
        check_vma=False,
    )
```

```python
import jax
import jax.numpy as jnp
from jax import lax
from jax.experimental import pallas as pl
from jax.experimental.pallas import tpu as pltpu
from jax.sharding import PartitionSpec as P

BLK = 128
GROUP = 4
INTERPRET = False


def con_sum(part, link_type):
    count = lax.axis_size("con")
    me = lax.axis_index("con")
    rows = part.shape[0]
    quarters = part.reshape((count, rows // count) + part.shape[1:])
    total = lax.dynamic_index_in_dim(quarters, me, 0, keepdims=False).astype(jnp.float32)
    for shift in range(1, count):
        pairs = [(i, (i + shift) % count) for i in range(count)]
        piece = lax.dynamic_index_in_dim(quarters, (me + shift) % count, 0, keepdims=False)
        total = total + lax.ppermute(piece.astype(link_type), "con", pairs).astype(jnp.float32)
    mine = total.astype(link_type)
    pieces = [mine]
    for shift in range(1, count):
        pairs = [(i, (i + shift) % count) for i in range(count)]
        pieces.append(lax.ppermute(mine, "con", pairs))
    slots = []
    for q in range(count):
        source = (me - q) % count
        slot = pieces[0]
        for shift in range(1, count):
            slot = jnp.where(source == shift, pieces[shift], slot)
        slots.append(slot)
    return jnp.concatenate(slots, axis=0).astype(jnp.float32)


def x_solve_kernel(s_ref, w_ref, o_ref):
    for b in range(w_ref.shape[0]):
        block = s_ref[:, b * BLK:(b + 1) * BLK]
        out = lax.dot_general(w_ref[b], block, (((1,), (1,)), ((), ())), preferred_element_type=jnp.float32)
        o_ref[b * BLK:(b + 1) * BLK, :] = out.astype(o_ref.dtype)


def x_solve(rows, inv_x):
    lanes, side = rows.shape
    nblocks = inv_x.shape[0]
    return pl.pallas_call(
        x_solve_kernel,
        grid=(nblocks // GROUP,),
        in_specs=[
            pl.BlockSpec((lanes, GROUP * BLK), lambda g: (0, g)),
            pl.BlockSpec((GROUP, BLK, BLK), lambda g: (g, 0, 0)),
        ],
        out_specs=pl.BlockSpec((GROUP * BLK, lanes), lambda g: (g, 0)),
        out_shape=jax.ShapeDtypeStruct((side, lanes), jnp.bfloat16),
        interpret=INTERPRET,
    )(rows, inv_x)


def y_solve_kernel(r_ref, m_ref, w_ref, v_ref, g_ref, i_ref):
    half = r_ref.shape[0] // (2 * w_ref.shape[0])
    count = v_ref.shape[0]
    lane = lax.broadcasted_iota(jnp.int32, (half, BLK), 1)
    low = lane < half
    for b in range(w_ref.shape[0]):
        cols = slice(b * BLK, (b + 1) * BLK)
        sea = m_ref[:, cols] == 1
        weight = w_ref[b]
        total = jnp.zeros((half, BLK), jnp.float32)
        for q in range(count):
            tile = slice((q // 2) * BLK, (q // 2 + 1) * BLK)
            first = r_ref[2 * b * half:(2 * b + 1) * half, tile].astype(jnp.float32)
            second = r_ref[(2 * b + 1) * half:(2 * b + 2) * half, tile].astype(jnp.float32)
            if q % 2 == 0:
                joined = jnp.where(low, first, pltpu.roll(second, half, 1))
            else:
                joined = jnp.where(low, pltpu.roll(first, half, 1), second)
            joined = jnp.where(sea, joined, 0.0).astype(jnp.bfloat16)
            out = lax.dot_general(joined, weight, (((1,), (1,)), ((), ())), preferred_element_type=jnp.float32)
            g_ref[q, :, cols] = out
            total = total + out * v_ref[q, :, cols].astype(jnp.float32)
        i_ref[:, cols] = total


def y_solve(arrived, land_mask, inv_y, vel):
    count, rows_local, side = vel.shape
    nblocks = inv_y.shape[0]
    return pl.pallas_call(
        y_solve_kernel,
        grid=(nblocks // GROUP,),
        in_specs=[
            pl.BlockSpec((GROUP * 2 * rows_local, arrived.shape[1]), lambda g: (g, 0)),
            pl.BlockSpec((rows_local, GROUP * BLK), lambda g: (0, g)),
            pl.BlockSpec((GROUP, BLK, BLK), lambda g: (g, 0, 0)),
            pl.BlockSpec((count, rows_local, GROUP * BLK), lambda g: (0, 0, g)),
        ],
        out_specs=[
            pl.BlockSpec((count, rows_local, GROUP * BLK), lambda g: (0, 0, g)),
            pl.BlockSpec((rows_local, GROUP * BLK), lambda g: (0, g)),
        ],
        out_shape=[
            jax.ShapeDtypeStruct((count, rows_local, side), jnp.float32),
            jax.ShapeDtypeStruct((rows_local, side), jnp.float32),
        ],
        interpret=INTERPRET,
    )(arrived, land_mask, inv_y, vel)


def local(velocity, seed_adjoint, land_mask, inv_x, inv_y, weights):
    con_local = velocity.shape[0]
    cols_local = seed_adjoint.shape[2]
    full_side = seed_adjoint.shape[3]
    rows_local = velocity.shape[2]
    vel_float = velocity.astype(jnp.float32)
    weight_full = weights[:, None, None, None]
    local_squares = jnp.sum(weight_full * vel_float * vel_float, axis=(0, 1))
    sea_float = (land_mask == 1).astype(jnp.float32)
    seed_rows = seed_adjoint.reshape(con_local, 2 * cols_local, full_side)
    vel_rows = velocity.reshape(con_local, 2, rows_local, full_side)
    landed = []
    for c in range(con_local):
        across = x_solve(seed_rows[c], inv_x)
        landed.append(lax.all_to_all(across, "grid", split_axis=0, concat_axis=0, tiled=True))
    landed[-1], local_squares = lax.optimization_barrier((landed[-1], local_squares))
    squares = con_sum(local_squares, jnp.bfloat16)
    solved_parts = []
    local_inner = None
    for c in range(con_local):
        part, part_inner = y_solve(landed[c], land_mask, inv_y, vel_rows[c])
        solved_parts.append(part)
        local_inner = part_inner if local_inner is None else local_inner + part_inner
    rhs_adjoint = jnp.stack(solved_parts, axis=0)
    inner = con_sum(local_inner, jnp.bfloat16)
    speed = jnp.sqrt(0.25 + squares)
    first = -0.5 * sea_float * speed * rhs_adjoint
    second = -0.5 * sea_float * weight_full * vel_float * inner / speed
    return first + second


def solution(mesh):
    return jax.shard_map(
        local,
        mesh=mesh,
        in_specs=(
            P("con", None, "grid", None),
            P("con", None, "grid", None),
            P("grid", None),
            P(),
            P(),
            P("con"),
        ),
        out_specs=P("con", None, "grid", None),
        check_vma=False,
    )
```

```python
import jax
import jax.numpy as jnp
from jax import lax
from jax.experimental import pallas as pl
from jax.experimental.pallas import tpu as pltpu
from jax.sharding import PartitionSpec as P

BLK = 128
GROUP = 8
INTERPRET = False


def con_sum(part, link_type):
    count = lax.axis_size("con")
    me = lax.axis_index("con")
    rows = part.shape[0]
    quarters = part.reshape((count, rows // count) + part.shape[1:])
    total = lax.dynamic_index_in_dim(quarters, me, 0, keepdims=False).astype(jnp.float32)
    for shift in range(1, count):
        pairs = [(i, (i + shift) % count) for i in range(count)]
        piece = lax.dynamic_index_in_dim(quarters, (me + shift) % count, 0, keepdims=False)
        total = total + lax.ppermute(piece.astype(link_type), "con", pairs).astype(jnp.float32)
    mine = total.astype(link_type)
    pieces = [mine]
    for shift in range(1, count):
        pairs = [(i, (i + shift) % count) for i in range(count)]
        pieces.append(lax.ppermute(mine, "con", pairs))
    slots = []
    for q in range(count):
        source = (me - q) % count
        slot = pieces[0]
        for shift in range(1, count):
            slot = jnp.where(source == shift, pieces[shift], slot)
        slots.append(slot)
    return jnp.concatenate(slots, axis=0).astype(jnp.float32)


def x_solve_kernel(s_ref, w_ref, o_ref):
    for b in range(w_ref.shape[0]):
        block = s_ref[:, b * BLK:(b + 1) * BLK]
        out = lax.dot_general(w_ref[b], block, (((1,), (1,)), ((), ())), preferred_element_type=jnp.float32)
        o_ref[b * BLK:(b + 1) * BLK, :] = out.astype(o_ref.dtype)


def x_solve(rows, inv_x):
    lanes, side = rows.shape
    nblocks = inv_x.shape[0]
    return pl.pallas_call(
        x_solve_kernel,
        grid=(nblocks // GROUP,),
        in_specs=[
            pl.BlockSpec((lanes, GROUP * BLK), lambda g: (0, g)),
            pl.BlockSpec((GROUP, BLK, BLK), lambda g: (g, 0, 0)),
        ],
        out_specs=pl.BlockSpec((GROUP * BLK, lanes), lambda g: (g, 0)),
        out_shape=jax.ShapeDtypeStruct((side, lanes), jnp.bfloat16),
        interpret=INTERPRET,
    )(rows, inv_x)


def y_solve_kernel(r_ref, m_ref, w_ref, v_ref, g_ref, i_ref):
    half = r_ref.shape[0] // (2 * w_ref.shape[0])
    count = v_ref.shape[0]
    lane = lax.broadcasted_iota(jnp.int32, (half, BLK), 1)
    low = lane < half
    for b in range(w_ref.shape[0]):
        cols = slice(b * BLK, (b + 1) * BLK)
        sea = m_ref[:, cols] == 1
        weight = w_ref[b]
        total = jnp.zeros((half, BLK), jnp.float32)
        for q in range(count):
            tile = slice((q // 2) * BLK, (q // 2 + 1) * BLK)
            first = r_ref[2 * b * half:(2 * b + 1) * half, tile]
            second = r_ref[(2 * b + 1) * half:(2 * b + 2) * half, tile]
            if q % 2 == 0:
                joined = jnp.where(low, first, pltpu.roll(second, half, 1))
            else:
                joined = jnp.where(low, pltpu.roll(first, half, 1), second)
            joined = jnp.where(sea, joined, jnp.zeros_like(joined))
            out = lax.dot_general(joined, weight, (((1,), (1,)), ((), ())), preferred_element_type=jnp.float32)
            g_ref[q, :, cols] = out
            total = total + out * v_ref[q, :, cols].astype(jnp.float32)
        i_ref[:, cols] = total


def y_solve(arrived, land_mask, inv_y, vel):
    count, rows_local, side = vel.shape
    nblocks = inv_y.shape[0]
    return pl.pallas_call(
        y_solve_kernel,
        grid=(nblocks // GROUP,),
        in_specs=[
            pl.BlockSpec((GROUP * 2 * rows_local, arrived.shape[1]), lambda g: (g, 0)),
            pl.BlockSpec((rows_local, GROUP * BLK), lambda g: (0, g)),
            pl.BlockSpec((GROUP, BLK, BLK), lambda g: (g, 0, 0)),
            pl.BlockSpec((count, rows_local, GROUP * BLK), lambda g: (0, 0, g)),
        ],
        out_specs=[
            pl.BlockSpec((count, rows_local, GROUP * BLK), lambda g: (0, 0, g)),
            pl.BlockSpec((rows_local, GROUP * BLK), lambda g: (0, g)),
        ],
        out_shape=[
            jax.ShapeDtypeStruct((count, rows_local, side), jnp.float32),
            jax.ShapeDtypeStruct((rows_local, side), jnp.float32),
        ],
        interpret=INTERPRET,
    )(arrived, land_mask, inv_y, vel)


def local(velocity, seed_adjoint, land_mask, inv_x, inv_y, weights):
    con_local = velocity.shape[0]
    cols_local = seed_adjoint.shape[2]
    full_side = seed_adjoint.shape[3]
    rows_local = velocity.shape[2]
    vel_float = velocity.astype(jnp.float32)
    weight_full = weights[:, None, None, None]
    local_squares = jnp.sum(weight_full * vel_float * vel_float, axis=(0, 1))
    sea_float = (land_mask == 1).astype(jnp.float32)
    across = x_solve(seed_adjoint.reshape(con_local * 2 * cols_local, full_side), inv_x)
    arrived = lax.all_to_all(across, "grid", split_axis=0, concat_axis=0, tiled=True)
    arrived, local_squares = lax.optimization_barrier((arrived, local_squares))
    squares = con_sum(local_squares, jnp.bfloat16)
    solved, local_inner = y_solve(arrived, land_mask, inv_y, velocity.reshape(con_local * 2, rows_local, full_side))
    rhs_adjoint = solved.reshape(con_local, 2, rows_local, full_side)
    inner = con_sum(local_inner, jnp.bfloat16)
    speed = jnp.sqrt(0.25 + squares)
    first = -0.5 * sea_float * speed * rhs_adjoint
    second = -0.5 * sea_float * weight_full * vel_float * inner / speed
    return first + second


def solution(mesh):
    return jax.shard_map(
        local,
        mesh=mesh,
        in_specs=(
            P("con", None, "grid", None),
            P("con", None, "grid", None),
            P("grid", None),
            P(),
            P(),
            P("con"),
        ),
        out_specs=P("con", None, "grid", None),
        check_vma=False,
    )
```

```python
import jax
import jax.numpy as jnp
from jax import lax
from jax.experimental import pallas as pl
from jax.experimental.pallas import tpu as pltpu
from jax.sharding import PartitionSpec as P

BLK = 128
GROUP = 16
INTERPRET = False


def con_sum(part, link_type):
    count = lax.axis_size("con")
    me = lax.axis_index("con")
    rows = part.shape[0]
    quarters = part.reshape((count, rows // count) + part.shape[1:])
    total = lax.dynamic_index_in_dim(quarters, me, 0, keepdims=False).astype(jnp.float32)
    for shift in range(1, count):
        pairs = [(i, (i + shift) % count) for i in range(count)]
        piece = lax.dynamic_index_in_dim(quarters, (me + shift) % count, 0, keepdims=False)
        total = total + lax.ppermute(piece.astype(link_type), "con", pairs).astype(jnp.float32)
    mine = total.astype(link_type)
    pieces = [mine]
    for shift in range(1, count):
        pairs = [(i, (i + shift) % count) for i in range(count)]
        pieces.append(lax.ppermute(mine, "con", pairs))
    slots = []
    for q in range(count):
        source = (me - q) % count
        slot = pieces[0]
        for shift in range(1, count):
            slot = jnp.where(source == shift, pieces[shift], slot)
        slots.append(slot)
    return jnp.concatenate(slots, axis=0).astype(jnp.float32)


def x_solve_kernel(s_ref, w_ref, o_ref):
    for b in range(w_ref.shape[0]):
        block = s_ref[:, b * BLK:(b + 1) * BLK]
        out = lax.dot_general(w_ref[b], block, (((1,), (1,)), ((), ())), preferred_element_type=jnp.float32)
        o_ref[b * BLK:(b + 1) * BLK, :] = out.astype(o_ref.dtype)


def x_solve(rows, inv_x):
    lanes, side = rows.shape
    nblocks = inv_x.shape[0]
    return pl.pallas_call(
        x_solve_kernel,
        grid=(nblocks // GROUP,),
        in_specs=[
            pl.BlockSpec((lanes, GROUP * BLK), lambda g: (0, g)),
            pl.BlockSpec((GROUP, BLK, BLK), lambda g: (g, 0, 0)),
        ],
        out_specs=pl.BlockSpec((GROUP * BLK, lanes), lambda g: (g, 0)),
        out_shape=jax.ShapeDtypeStruct((side, lanes), jnp.bfloat16),
        interpret=INTERPRET,
    )(rows, inv_x)


def y_solve_kernel(r_ref, m_ref, w_ref, v_ref, g_ref, i_ref):
    half = r_ref.shape[0] // (2 * w_ref.shape[0])
    count = v_ref.shape[0]
    lane = lax.broadcasted_iota(jnp.int32, (half, BLK), 1)
    low = lane < half
    for b in range(w_ref.shape[0]):
        cols = slice(b * BLK, (b + 1) * BLK)
        sea = m_ref[:, cols] == 1
        weight = w_ref[b]
        total = jnp.zeros((half, BLK), jnp.float32)
        for q in range(count):
            tile = slice((q // 2) * BLK, (q // 2 + 1) * BLK)
            first = r_ref[2 * b * half:(2 * b + 1) * half, tile]
            second = r_ref[(2 * b + 1) * half:(2 * b + 2) * half, tile]
            if q % 2 == 0:
                joined = jnp.where(low, first, pltpu.roll(second, half, 1))
            else:
                joined = jnp.where(low, pltpu.roll(first, half, 1), second)
            joined = jnp.where(sea, joined, jnp.zeros_like(joined))
            out = lax.dot_general(joined, weight, (((1,), (1,)), ((), ())), preferred_element_type=jnp.float32)
            g_ref[q, :, cols] = out
            total = total + out * v_ref[q, :, cols].astype(jnp.float32)
        i_ref[:, cols] = total


def y_solve(arrived, land_mask, inv_y, vel):
    count, rows_local, side = vel.shape
    nblocks = inv_y.shape[0]
    return pl.pallas_call(
        y_solve_kernel,
        grid=(nblocks // GROUP,),
        in_specs=[
            pl.BlockSpec((GROUP * 2 * rows_local, arrived.shape[1]), lambda g: (g, 0)),
            pl.BlockSpec((rows_local, GROUP * BLK), lambda g: (0, g)),
            pl.BlockSpec((GROUP, BLK, BLK), lambda g: (g, 0, 0)),
            pl.BlockSpec((count, rows_local, GROUP * BLK), lambda g: (0, 0, g)),
        ],
        out_specs=[
            pl.BlockSpec((count, rows_local, GROUP * BLK), lambda g: (0, 0, g)),
            pl.BlockSpec((rows_local, GROUP * BLK), lambda g: (0, g)),
        ],
        out_shape=[
            jax.ShapeDtypeStruct((count, rows_local, side), jnp.float32),
            jax.ShapeDtypeStruct((rows_local, side), jnp.float32),
        ],
        interpret=INTERPRET,
    )(arrived, land_mask, inv_y, vel)


def local(velocity, seed_adjoint, land_mask, inv_x, inv_y, weights):
    con_local = velocity.shape[0]
    cols_local = seed_adjoint.shape[2]
    full_side = seed_adjoint.shape[3]
    rows_local = velocity.shape[2]
    vel_float = velocity.astype(jnp.float32)
    weight_full = weights[:, None, None, None]
    local_squares = jnp.sum(weight_full * vel_float * vel_float, axis=(0, 1))
    sea_float = (land_mask == 1).astype(jnp.float32)
    across = x_solve(seed_adjoint.reshape(con_local * 2 * cols_local, full_side), inv_x)
    arrived = lax.all_to_all(across, "grid", split_axis=0, concat_axis=0, tiled=True)
    arrived, local_squares = lax.optimization_barrier((arrived, local_squares))
    squares = con_sum(local_squares, jnp.bfloat16)
    solved, local_inner = y_solve(arrived, land_mask, inv_y, velocity.reshape(con_local * 2, rows_local, full_side))
    rhs_adjoint = solved.reshape(con_local, 2, rows_local, full_side)
    inner = con_sum(local_inner, jnp.bfloat16)
    speed = jnp.sqrt(0.25 + squares)
    first = -0.5 * sea_float * speed * rhs_adjoint
    second = -0.5 * sea_float * weight_full * vel_float * inner / speed
    return first + second


def solution(mesh):
    return jax.shard_map(
        local,
        mesh=mesh,
        in_specs=(
            P("con", None, "grid", None),
            P("con", None, "grid", None),
            P("grid", None),
            P(),
            P(),
            P("con"),
        ),
        out_specs=P("con", None, "grid", None),
        check_vma=False,
    )
```

```python
import jax
import jax.numpy as jnp
from jax import lax
from jax.experimental import pallas as pl
from jax.experimental.pallas import tpu as pltpu
from jax.sharding import PartitionSpec as P

BLK = 128
GROUP = 16
INTERPRET = False


def con_pairs(shift):
    count = lax.axis_size("con")
    return [(i, (i + shift) % count) for i in range(count)]


def con_scatter(part, link_type):
    count = lax.axis_size("con")
    me = lax.axis_index("con")
    rows = part.shape[0]
    quarters = part.reshape((count, rows // count) + part.shape[1:])
    total = lax.dynamic_index_in_dim(quarters, me, 0, keepdims=False).astype(jnp.float32)
    for shift in range(1, count):
        piece = lax.dynamic_index_in_dim(quarters, (me + shift) % count, 0, keepdims=False)
        total = total + lax.ppermute(piece.astype(link_type), "con", con_pairs(shift)).astype(jnp.float32)
    return total.astype(link_type)


def con_gather(mine, axis):
    count = lax.axis_size("con")
    me = lax.axis_index("con")
    pieces = [mine] + [lax.ppermute(mine, "con", con_pairs(shift)) for shift in range(1, count)]
    slots = []
    for q in range(count):
        source = (me - q) % count
        slot = pieces[0]
        for shift in range(1, count):
            slot = jnp.where(source == shift, pieces[shift], slot)
        slots.append(slot)
    return jnp.concatenate(slots, axis=axis).astype(jnp.float32)


def x_solve_kernel(s_ref, w_ref, o_ref):
    for b in range(w_ref.shape[0]):
        block = s_ref[:, b * BLK:(b + 1) * BLK]
        out = lax.dot_general(w_ref[b], block, (((1,), (1,)), ((), ())), preferred_element_type=jnp.float32)
        o_ref[b * BLK:(b + 1) * BLK, :] = out.astype(o_ref.dtype)


def x_solve(rows, inv_x):
    lanes, side = rows.shape
    nblocks = inv_x.shape[0]
    return pl.pallas_call(
        x_solve_kernel,
        grid=(nblocks // GROUP,),
        in_specs=[
            pl.BlockSpec((lanes, GROUP * BLK), lambda g: (0, g)),
            pl.BlockSpec((GROUP, BLK, BLK), lambda g: (g, 0, 0)),
        ],
        out_specs=pl.BlockSpec((GROUP * BLK, lanes), lambda g: (g, 0)),
        out_shape=jax.ShapeDtypeStruct((side, lanes), jnp.bfloat16),
        interpret=INTERPRET,
    )(rows, inv_x)


def y_solve_kernel(r_ref, m_ref, w_ref, v_ref, g_ref, i_ref):
    half = r_ref.shape[0] // (2 * w_ref.shape[0])
    count = v_ref.shape[0]
    lane = lax.broadcasted_iota(jnp.int32, (half, BLK), 1)
    low = lane < half
    for b in range(w_ref.shape[0]):
        cols = slice(b * BLK, (b + 1) * BLK)
        sea = m_ref[:, cols] == 1
        weight = w_ref[b]
        total = jnp.zeros((half, BLK), jnp.float32)
        for q in range(count):
            tile = slice((q // 2) * BLK, (q // 2 + 1) * BLK)
            first = r_ref[2 * b * half:(2 * b + 1) * half, tile]
            second = r_ref[(2 * b + 1) * half:(2 * b + 2) * half, tile]
            if q % 2 == 0:
                joined = jnp.where(low, first, pltpu.roll(second, half, 1))
            else:
                joined = jnp.where(low, pltpu.roll(first, half, 1), second)
            joined = jnp.where(sea, joined, jnp.zeros_like(joined))
            out = lax.dot_general(joined, weight, (((1,), (1,)), ((), ())), preferred_element_type=jnp.float32)
            g_ref[q, :, cols] = out
            total = total + out * v_ref[q, :, cols].astype(jnp.float32)
        i_ref[:, cols] = total


def y_solve(arrived, land_mask, inv_y, vel):
    count, rows_local, side = vel.shape
    nblocks = inv_y.shape[0]
    return pl.pallas_call(
        y_solve_kernel,
        grid=(nblocks // GROUP,),
        in_specs=[
            pl.BlockSpec((GROUP * 2 * rows_local, arrived.shape[1]), lambda g: (g, 0)),
            pl.BlockSpec((rows_local, GROUP * BLK), lambda g: (0, g)),
            pl.BlockSpec((GROUP, BLK, BLK), lambda g: (g, 0, 0)),
            pl.BlockSpec((count, rows_local, GROUP * BLK), lambda g: (0, 0, g)),
        ],
        out_specs=[
            pl.BlockSpec((count, rows_local, GROUP * BLK), lambda g: (0, 0, g)),
            pl.BlockSpec((rows_local, GROUP * BLK), lambda g: (0, g)),
        ],
        out_shape=[
            jax.ShapeDtypeStruct((count, rows_local, side), jnp.float32),
            jax.ShapeDtypeStruct((rows_local, side), jnp.float32),
        ],
        interpret=INTERPRET,
    )(arrived, land_mask, inv_y, vel)


def local(velocity, seed_adjoint, land_mask, inv_x, inv_y, weights):
    con_local = velocity.shape[0]
    cols_local = seed_adjoint.shape[2]
    full_side = seed_adjoint.shape[3]
    rows_local = velocity.shape[2]
    vel_float = velocity.astype(jnp.float32)
    weight_full = weights[:, None, None, None]
    local_squares = jnp.sum(weight_full * vel_float * vel_float, axis=(0, 1))
    sea_float = (land_mask == 1).astype(jnp.float32)
    across = x_solve(seed_adjoint.reshape(con_local * 2 * cols_local, full_side), inv_x)
    arrived = lax.all_to_all(across, "grid", split_axis=0, concat_axis=0, tiled=True)
    arrived, local_squares = lax.optimization_barrier((arrived, local_squares))
    squares_mine = con_scatter(local_squares, jnp.bfloat16)
    solved, local_inner = y_solve(arrived, land_mask, inv_y, velocity.reshape(con_local * 2, rows_local, full_side))
    rhs_adjoint = solved.reshape(con_local, 2, rows_local, full_side)
    inner_mine = con_scatter(local_inner, jnp.bfloat16)
    squares, inner = con_gather(jnp.stack([squares_mine, inner_mine]), axis=1)
    speed = jnp.sqrt(0.25 + squares)
    first = -0.5 * sea_float * speed * rhs_adjoint
    second = -0.5 * sea_float * weight_full * vel_float * inner / speed
    return first + second


def solution(mesh):
    return jax.shard_map(
        local,
        mesh=mesh,
        in_specs=(
            P("con", None, "grid", None),
            P("con", None, "grid", None),
            P("grid", None),
            P(),
            P(),
            P("con"),
        ),
        out_specs=P("con", None, "grid", None),
        check_vma=False,
    )
```

```python
import jax
import jax.numpy as jnp
from jax import lax
from jax.experimental import pallas as pl
from jax.experimental.pallas import tpu as pltpu
from jax.sharding import PartitionSpec as P

BLK = 128
GROUP = 16
INTERPRET = False


def con_sum(part, link_type):
    count = lax.axis_size("con")
    me = lax.axis_index("con")
    rows = part.shape[0]
    quarters = part.reshape((count, rows // count) + part.shape[1:])
    total = lax.dynamic_index_in_dim(quarters, me, 0, keepdims=False).astype(jnp.float32)
    for shift in range(1, count):
        pairs = [(i, (i + shift) % count) for i in range(count)]
        piece = lax.dynamic_index_in_dim(quarters, (me + shift) % count, 0, keepdims=False)
        total = total + lax.ppermute(piece.astype(link_type), "con", pairs).astype(jnp.float32)
    mine = total.astype(link_type)
    pieces = [mine]
    for shift in range(1, count):
        pairs = [(i, (i + shift) % count) for i in range(count)]
        pieces.append(lax.ppermute(mine, "con", pairs))
    slots = []
    for q in range(count):
        source = (me - q) % count
        slot = pieces[0]
        for shift in range(1, count):
            slot = jnp.where(source == shift, pieces[shift], slot)
        slots.append(slot)
    return jnp.concatenate(slots, axis=0).astype(jnp.float32)


def x_solve_kernel(s_ref, w_ref, o_ref):
    for b in range(w_ref.shape[0]):
        block = s_ref[:, b * BLK:(b + 1) * BLK]
        out = lax.dot_general(w_ref[b], block, (((1,), (1,)), ((), ())), preferred_element_type=jnp.float32)
        o_ref[b * BLK:(b + 1) * BLK, :] = out.astype(o_ref.dtype)


def x_solve(rows, inv_x):
    lanes, side = rows.shape
    nblocks = inv_x.shape[0]
    return pl.pallas_call(
        x_solve_kernel,
        grid=(nblocks // GROUP,),
        in_specs=[
            pl.BlockSpec((lanes, GROUP * BLK), lambda g: (0, g)),
            pl.BlockSpec((GROUP, BLK, BLK), lambda g: (g, 0, 0)),
        ],
        out_specs=pl.BlockSpec((GROUP * BLK, lanes), lambda g: (g, 0)),
        out_shape=jax.ShapeDtypeStruct((side, lanes), jnp.bfloat16),
        interpret=INTERPRET,
    )(rows, inv_x)


def y_solve_kernel(r_ref, m_ref, w_ref, v_ref, g_ref, i_ref):
    half = r_ref.shape[0] // (2 * w_ref.shape[0])
    count = v_ref.shape[0]
    lane = lax.broadcasted_iota(jnp.int32, (half, BLK), 1)
    low = lane < half
    for b in range(w_ref.shape[0]):
        cols = slice(b * BLK, (b + 1) * BLK)
        sea = m_ref[:, cols] == 1
        weight = w_ref[b]
        total = jnp.zeros((half, BLK), jnp.float32)
        for q in range(count):
            tile = slice((q // 2) * BLK, (q // 2 + 1) * BLK)
            first = r_ref[2 * b * half:(2 * b + 1) * half, tile]
            second = r_ref[(2 * b + 1) * half:(2 * b + 2) * half, tile]
            if q % 2 == 0:
                joined = jnp.where(low, first, pltpu.roll(second, half, 1))
            else:
                joined = jnp.where(low, pltpu.roll(first, half, 1), second)
            joined = jnp.where(sea, joined, jnp.zeros_like(joined))
            out = lax.dot_general(joined, weight, (((1,), (1,)), ((), ())), preferred_element_type=jnp.float32)
            g_ref[q, :, cols] = out
            total = total + out * v_ref[q, :, cols].astype(jnp.float32)
        i_ref[:, cols] = total


def y_solve(arrived, land_mask, inv_y, vel):
    count, rows_local, side = vel.shape
    nblocks = inv_y.shape[0]
    return pl.pallas_call(
        y_solve_kernel,
        grid=(nblocks // GROUP,),
        in_specs=[
            pl.BlockSpec((GROUP * 2 * rows_local, arrived.shape[1]), lambda g: (g, 0)),
            pl.BlockSpec((rows_local, GROUP * BLK), lambda g: (0, g)),
            pl.BlockSpec((GROUP, BLK, BLK), lambda g: (g, 0, 0)),
            pl.BlockSpec((count, rows_local, GROUP * BLK), lambda g: (0, 0, g)),
        ],
        out_specs=[
            pl.BlockSpec((count, rows_local, GROUP * BLK), lambda g: (0, 0, g)),
            pl.BlockSpec((rows_local, GROUP * BLK), lambda g: (0, g)),
        ],
        out_shape=[
            jax.ShapeDtypeStruct((count, rows_local, side), jnp.float32),
            jax.ShapeDtypeStruct((rows_local, side), jnp.float32),
        ],
        interpret=INTERPRET,
    )(arrived, land_mask, inv_y, vel)


def local(velocity, seed_adjoint, land_mask, inv_x, inv_y, weights):
    con_local = velocity.shape[0]
    cols_local = seed_adjoint.shape[2]
    full_side = seed_adjoint.shape[3]
    rows_local = velocity.shape[2]
    vel_float = velocity.astype(jnp.float32)
    weight_full = weights[:, None, None, None]
    local_squares = jnp.sum(weight_full * vel_float * vel_float, axis=(0, 1))
    sea_float = (land_mask == 1).astype(jnp.float32)
    across = x_solve(seed_adjoint.reshape(con_local * 2 * cols_local, full_side), inv_x)
    arrived = lax.all_to_all(across, "grid", split_axis=0, concat_axis=0, tiled=True)
    squares = lax.psum(local_squares.astype(jnp.bfloat16), "con").astype(jnp.float32)
    solved, local_inner = y_solve(arrived, land_mask, inv_y, velocity.reshape(con_local * 2, rows_local, full_side))
    rhs_adjoint = solved.reshape(con_local, 2, rows_local, full_side)
    inner = con_sum(local_inner, jnp.bfloat16)
    speed = jnp.sqrt(0.25 + squares)
    first = -0.5 * sea_float * speed * rhs_adjoint
    second = -0.5 * sea_float * weight_full * vel_float * inner / speed
    return first + second


def solution(mesh):
    return jax.shard_map(
        local,
        mesh=mesh,
        in_specs=(
            P("con", None, "grid", None),
            P("con", None, "grid", None),
            P("grid", None),
            P(),
            P(),
            P("con"),
        ),
        out_specs=P("con", None, "grid", None),
        check_vma=False,
    )
```

```python
import jax
import jax.numpy as jnp
from jax import lax
from jax.experimental import pallas as pl
from jax.experimental.pallas import tpu as pltpu
from jax.sharding import PartitionSpec as P

BLK = 128
GROUP = 16
INTERPRET = False


def con_sum(part, link_type):
    count = lax.axis_size("con")
    me = lax.axis_index("con")
    rows = part.shape[0]
    quarters = part.reshape((count, rows // count) + part.shape[1:])
    total = lax.dynamic_index_in_dim(quarters, me, 0, keepdims=False).astype(jnp.float32)
    for shift in range(1, count):
        pairs = [(i, (i + shift) % count) for i in range(count)]
        piece = lax.dynamic_index_in_dim(quarters, (me + shift) % count, 0, keepdims=False)
        total = total + lax.ppermute(piece.astype(link_type), "con", pairs).astype(jnp.float32)
    mine = total.astype(link_type)
    pieces = [mine]
    for shift in range(1, count):
        pairs = [(i, (i + shift) % count) for i in range(count)]
        pieces.append(lax.ppermute(mine, "con", pairs))
    slots = []
    for q in range(count):
        source = (me - q) % count
        slot = pieces[0]
        for shift in range(1, count):
            slot = jnp.where(source == shift, pieces[shift], slot)
        slots.append(slot)
    return jnp.concatenate(slots, axis=0).astype(jnp.float32)


def x_solve_kernel(s_ref, w_ref, o_ref):
    for b in range(w_ref.shape[0]):
        block = s_ref[:, b * BLK:(b + 1) * BLK]
        out = lax.dot_general(w_ref[b], block, (((1,), (1,)), ((), ())), preferred_element_type=jnp.float32)
        o_ref[b * BLK:(b + 1) * BLK, :] = out.astype(o_ref.dtype)


def x_solve(rows, inv_x):
    lanes, side = rows.shape
    nblocks = inv_x.shape[0]
    return pl.pallas_call(
        x_solve_kernel,
        grid=(nblocks // GROUP,),
        in_specs=[
            pl.BlockSpec((lanes, GROUP * BLK), lambda g: (0, g)),
            pl.BlockSpec((GROUP, BLK, BLK), lambda g: (g, 0, 0)),
        ],
        out_specs=pl.BlockSpec((GROUP * BLK, lanes), lambda g: (g, 0)),
        out_shape=jax.ShapeDtypeStruct((side, lanes), jnp.bfloat16),
        interpret=INTERPRET,
    )(rows, inv_x)


def y_solve_kernel(r_ref, m_ref, w_ref, v_ref, g_ref, i_ref):
    half = r_ref.shape[0] // (2 * w_ref.shape[0])
    count = v_ref.shape[0]
    lane = lax.broadcasted_iota(jnp.int32, (half, BLK), 1)
    low = lane < half
    for b in range(w_ref.shape[0]):
        cols = slice(b * BLK, (b + 1) * BLK)
        sea = m_ref[:, cols] == 1
        weight = w_ref[b]
        total = jnp.zeros((half, BLK), jnp.float32)
        for q in range(count):
            tile = slice((q // 2) * BLK, (q // 2 + 1) * BLK)
            first = r_ref[2 * b * half:(2 * b + 1) * half, tile]
            second = r_ref[(2 * b + 1) * half:(2 * b + 2) * half, tile]
            if q % 2 == 0:
                joined = jnp.where(low, first, pltpu.roll(second, half, 1))
            else:
                joined = jnp.where(low, pltpu.roll(first, half, 1), second)
            joined = jnp.where(sea, joined, jnp.zeros_like(joined))
            out = lax.dot_general(joined, weight, (((1,), (1,)), ((), ())), preferred_element_type=jnp.float32)
            g_ref[q, :, cols] = out
            total = total + out * v_ref[q, :, cols].astype(jnp.float32)
        i_ref[:, cols] = total


def y_solve(arrived, land_mask, inv_y, vel):
    count, rows_local, side = vel.shape
    nblocks = inv_y.shape[0]
    return pl.pallas_call(
        y_solve_kernel,
        grid=(nblocks // GROUP,),
        in_specs=[
            pl.BlockSpec((GROUP * 2 * rows_local, arrived.shape[1]), lambda g: (g, 0)),
            pl.BlockSpec((rows_local, GROUP * BLK), lambda g: (0, g)),
            pl.BlockSpec((GROUP, BLK, BLK), lambda g: (g, 0, 0)),
            pl.BlockSpec((count, rows_local, GROUP * BLK), lambda g: (0, 0, g)),
        ],
        out_specs=[
            pl.BlockSpec((count, rows_local, GROUP * BLK), lambda g: (0, 0, g)),
            pl.BlockSpec((rows_local, GROUP * BLK), lambda g: (0, g)),
        ],
        out_shape=[
            jax.ShapeDtypeStruct((count, rows_local, side), jnp.float32),
            jax.ShapeDtypeStruct((rows_local, side), jnp.float32),
        ],
        interpret=INTERPRET,
    )(arrived, land_mask, inv_y, vel)


def local(velocity, seed_adjoint, land_mask, inv_x, inv_y, weights):
    con_local = velocity.shape[0]
    cols_local = seed_adjoint.shape[2]
    full_side = seed_adjoint.shape[3]
    rows_local = velocity.shape[2]
    vel_float = velocity.astype(jnp.float32)
    weight_full = weights[:, None, None, None]
    local_squares = jnp.sum(weight_full * vel_float * vel_float, axis=(0, 1))
    sea_float = (land_mask == 1).astype(jnp.float32)
    across = x_solve(seed_adjoint.reshape(con_local * 2 * cols_local, full_side), inv_x)
    arrived = lax.all_to_all(across, "grid", split_axis=0, concat_axis=0, tiled=True)
    solved, local_inner = y_solve(arrived, land_mask, inv_y, velocity.reshape(con_local * 2, rows_local, full_side))
    rhs_adjoint = solved.reshape(con_local, 2, rows_local, full_side)
    local_inner, local_squares = lax.optimization_barrier((local_inner, local_squares))
    squares = con_sum(local_squares, jnp.bfloat16)
    inner = con_sum(local_inner, jnp.bfloat16)
    speed = jnp.sqrt(0.25 + squares)
    first = -0.5 * sea_float * speed * rhs_adjoint
    second = -0.5 * sea_float * weight_full * vel_float * inner / speed
    return first + second


def solution(mesh):
    return jax.shard_map(
        local,
        mesh=mesh,
        in_specs=(
            P("con", None, "grid", None),
            P("con", None, "grid", None),
            P("grid", None),
            P(),
            P(),
            P("con"),
        ),
        out_specs=P("con", None, "grid", None),
        check_vma=False,
    )
```

```python
import jax
import jax.numpy as jnp
from jax import lax
from jax.experimental import pallas as pl
from jax.experimental.pallas import tpu as pltpu
from jax.sharding import PartitionSpec as P

BLK = 128
GROUP = 16
INTERPRET = False


def con_pairs(shift):
    count = lax.axis_size("con")
    return [(i, (i + shift) % count) for i in range(count)]


def con_sum(part, link_type):
    count = lax.axis_size("con")
    me = lax.axis_index("con")
    rows = part.shape[0]
    size = rows // count
    half = size // 2
    quarters = part.astype(link_type).reshape((count, size) + part.shape[1:])

    def quarter(offset):
        return lax.dynamic_index_in_dim(quarters, (me + offset) % count, 0, keepdims=False)

    ahead, behind = con_pairs(1), con_pairs(count - 1)
    opposite = quarter(2)
    got_left = lax.ppermute(jnp.concatenate([quarter(1), opposite[:half]]), "con", ahead)
    got_right = lax.ppermute(jnp.concatenate([quarter(-1), opposite[half:]]), "con", behind)
    relayed_left = lax.ppermute(got_left[size:], "con", ahead)
    relayed_right = lax.ppermute(got_right[size:], "con", behind)
    total = (quarter(0).astype(jnp.float32) + got_left[:size].astype(jnp.float32)
             + got_right[:size].astype(jnp.float32)
             + jnp.concatenate([relayed_left, relayed_right]).astype(jnp.float32))
    mine = total.astype(link_type)
    from_left = lax.ppermute(mine, "con", ahead)
    from_right = lax.ppermute(mine, "con", behind)
    far = jnp.concatenate([lax.ppermute(from_left[:half], "con", ahead),
                           lax.ppermute(from_right[half:], "con", behind)])
    by_offset = [mine, from_right, far, from_left]
    slots = []
    for q in range(count):
        offset = (q - me) % count
        slot = by_offset[0]
        for k in range(1, count):
            slot = jnp.where(offset == k, by_offset[k], slot)
        slots.append(slot)
    return jnp.concatenate(slots, axis=0).astype(jnp.float32)


def x_solve_kernel(s_ref, w_ref, o_ref):
    for b in range(w_ref.shape[0]):
        block = s_ref[:, b * BLK:(b + 1) * BLK]
        out = lax.dot_general(w_ref[b], block, (((1,), (1,)), ((), ())), preferred_element_type=jnp.float32)
        o_ref[b * BLK:(b + 1) * BLK, :] = out.astype(o_ref.dtype)


def x_solve(rows, inv_x):
    lanes, side = rows.shape
    nblocks = inv_x.shape[0]
    return pl.pallas_call(
        x_solve_kernel,
        grid=(nblocks // GROUP,),
        in_specs=[
            pl.BlockSpec((lanes, GROUP * BLK), lambda g: (0, g)),
            pl.BlockSpec((GROUP, BLK, BLK), lambda g: (g, 0, 0)),
        ],
        out_specs=pl.BlockSpec((GROUP * BLK, lanes), lambda g: (g, 0)),
        out_shape=jax.ShapeDtypeStruct((side, lanes), jnp.bfloat16),
        interpret=INTERPRET,
    )(rows, inv_x)


def y_solve_kernel(r_ref, m_ref, w_ref, v_ref, g_ref, i_ref):
    half = r_ref.shape[0] // (2 * w_ref.shape[0])
    count = v_ref.shape[0]
    lane = lax.broadcasted_iota(jnp.int32, (half, BLK), 1)
    low = lane < half
    for b in range(w_ref.shape[0]):
        cols = slice(b * BLK, (b + 1) * BLK)
        sea = m_ref[:, cols] == 1
        weight = w_ref[b]
        total = jnp.zeros((half, BLK), jnp.float32)
        for q in range(count):
            tile = slice((q // 2) * BLK, (q // 2 + 1) * BLK)
            first = r_ref[2 * b * half:(2 * b + 1) * half, tile]
            second = r_ref[(2 * b + 1) * half:(2 * b + 2) * half, tile]
            if q % 2 == 0:
                joined = jnp.where(low, first, pltpu.roll(second, half, 1))
            else:
                joined = jnp.where(low, pltpu.roll(first, half, 1), second)
            joined = jnp.where(sea, joined, jnp.zeros_like(joined))
            out = lax.dot_general(joined, weight, (((1,), (1,)), ((), ())), preferred_element_type=jnp.float32)
            g_ref[q, :, cols] = out
            total = total + out * v_ref[q, :, cols].astype(jnp.float32)
        i_ref[:, cols] = total


def y_solve(arrived, land_mask, inv_y, vel):
    count, rows_local, side = vel.shape
    nblocks = inv_y.shape[0]
    return pl.pallas_call(
        y_solve_kernel,
        grid=(nblocks // GROUP,),
        in_specs=[
            pl.BlockSpec((GROUP * 2 * rows_local, arrived.shape[1]), lambda g: (g, 0)),
            pl.BlockSpec((rows_local, GROUP * BLK), lambda g: (0, g)),
            pl.BlockSpec((GROUP, BLK, BLK), lambda g: (g, 0, 0)),
            pl.BlockSpec((count, rows_local, GROUP * BLK), lambda g: (0, 0, g)),
        ],
        out_specs=[
            pl.BlockSpec((count, rows_local, GROUP * BLK), lambda g: (0, 0, g)),
            pl.BlockSpec((rows_local, GROUP * BLK), lambda g: (0, g)),
        ],
        out_shape=[
            jax.ShapeDtypeStruct((count, rows_local, side), jnp.float32),
            jax.ShapeDtypeStruct((rows_local, side), jnp.float32),
        ],
        interpret=INTERPRET,
    )(arrived, land_mask, inv_y, vel)


def local(velocity, seed_adjoint, land_mask, inv_x, inv_y, weights):
    con_local = velocity.shape[0]
    cols_local = seed_adjoint.shape[2]
    full_side = seed_adjoint.shape[3]
    rows_local = velocity.shape[2]
    vel_float = velocity.astype(jnp.float32)
    weight_full = weights[:, None, None, None]
    local_squares = jnp.sum(weight_full * vel_float * vel_float, axis=(0, 1))
    sea_float = (land_mask == 1).astype(jnp.float32)
    across = x_solve(seed_adjoint.reshape(con_local * 2 * cols_local, full_side), inv_x)
    arrived = lax.all_to_all(across, "grid", split_axis=0, concat_axis=0, tiled=True)
    arrived, local_squares = lax.optimization_barrier((arrived, local_squares))
    squares = con_sum(local_squares, jnp.bfloat16)
    solved, local_inner = y_solve(arrived, land_mask, inv_y, velocity.reshape(con_local * 2, rows_local, full_side))
    rhs_adjoint = solved.reshape(con_local, 2, rows_local, full_side)
    inner = con_sum(local_inner, jnp.bfloat16)
    speed = jnp.sqrt(0.25 + squares)
    first = -0.5 * sea_float * speed * rhs_adjoint
    second = -0.5 * sea_float * weight_full * vel_float * inner / speed
    return first + second


def solution(mesh):
    return jax.shard_map(
        local,
        mesh=mesh,
        in_specs=(
            P("con", None, "grid", None),
            P("con", None, "grid", None),
            P("grid", None),
            P(),
            P(),
            P("con"),
        ),
        out_specs=P("con", None, "grid", None),
        check_vma=False,
    )
```

```python
import jax
import jax.numpy as jnp
from jax import lax
from jax.experimental import pallas as pl
from jax.experimental.pallas import tpu as pltpu
from jax.sharding import PartitionSpec as P

BLK = 128
GROUP = 16
INTERPRET = False


def con_sum(part, link_type):
    count = lax.axis_size("con")
    me = lax.axis_index("con")
    rows = part.shape[0]
    quarters = part.reshape((count, rows // count) + part.shape[1:])
    total = lax.dynamic_index_in_dim(quarters, me, 0, keepdims=False).astype(jnp.float32)
    for shift in (2, 1, 3):
        pairs = [(i, (i + shift) % count) for i in range(count)]
        piece = lax.dynamic_index_in_dim(quarters, (me + shift) % count, 0, keepdims=False)
        total = total + lax.ppermute(piece.astype(link_type), "con", pairs).astype(jnp.float32)
    mine = total.astype(link_type)
    pieces = {0: mine}
    for shift in (2, 1, 3):
        pairs = [(i, (i + shift) % count) for i in range(count)]
        pieces[shift] = lax.ppermute(mine, "con", pairs)
    slots = []
    for q in range(count):
        source = (me - q) % count
        slot = pieces[0]
        for shift in range(1, count):
            slot = jnp.where(source == shift, pieces[shift], slot)
        slots.append(slot)
    return jnp.concatenate(slots, axis=0).astype(jnp.float32)


def x_solve_kernel(s_ref, w_ref, o_ref):
    for b in range(w_ref.shape[0]):
        block = s_ref[:, b * BLK:(b + 1) * BLK]
        out = lax.dot_general(w_ref[b], block, (((1,), (1,)), ((), ())), preferred_element_type=jnp.float32)
        o_ref[b * BLK:(b + 1) * BLK, :] = out.astype(o_ref.dtype)


def x_solve(rows, inv_x):
    lanes, side = rows.shape
    nblocks = inv_x.shape[0]
    return pl.pallas_call(
        x_solve_kernel,
        grid=(nblocks // GROUP,),
        in_specs=[
            pl.BlockSpec((lanes, GROUP * BLK), lambda g: (0, g)),
            pl.BlockSpec((GROUP, BLK, BLK), lambda g: (g, 0, 0)),
        ],
        out_specs=pl.BlockSpec((GROUP * BLK, lanes), lambda g: (g, 0)),
        out_shape=jax.ShapeDtypeStruct((side, lanes), jnp.bfloat16),
        interpret=INTERPRET,
    )(rows, inv_x)


def y_solve_kernel(r_ref, m_ref, w_ref, v_ref, g_ref, i_ref):
    half = r_ref.shape[0] // (2 * w_ref.shape[0])
    count = v_ref.shape[0]
    lane = lax.broadcasted_iota(jnp.int32, (half, BLK), 1)
    low = lane < half
    for b in range(w_ref.shape[0]):
        cols = slice(b * BLK, (b + 1) * BLK)
        sea = m_ref[:, cols] == 1
        weight = w_ref[b]
        total = jnp.zeros((half, BLK), jnp.float32)
        for q in range(count):
            tile = slice((q // 2) * BLK, (q // 2 + 1) * BLK)
            first = r_ref[2 * b * half:(2 * b + 1) * half, tile]
            second = r_ref[(2 * b + 1) * half:(2 * b + 2) * half, tile]
            if q % 2 == 0:
                joined = jnp.where(low, first, pltpu.roll(second, half, 1))
            else:
                joined = jnp.where(low, pltpu.roll(first, half, 1), second)
            joined = jnp.where(sea, joined, jnp.zeros_like(joined))
            out = lax.dot_general(joined, weight, (((1,), (1,)), ((), ())), preferred_element_type=jnp.float32)
            g_ref[q, :, cols] = out
            total = total + out * v_ref[q, :, cols].astype(jnp.float32)
        i_ref[:, cols] = total


def y_solve(arrived, land_mask, inv_y, vel):
    count, rows_local, side = vel.shape
    nblocks = inv_y.shape[0]
    return pl.pallas_call(
        y_solve_kernel,
        grid=(nblocks // GROUP,),
        in_specs=[
            pl.BlockSpec((GROUP * 2 * rows_local, arrived.shape[1]), lambda g: (g, 0)),
            pl.BlockSpec((rows_local, GROUP * BLK), lambda g: (0, g)),
            pl.BlockSpec((GROUP, BLK, BLK), lambda g: (g, 0, 0)),
            pl.BlockSpec((count, rows_local, GROUP * BLK), lambda g: (0, 0, g)),
        ],
        out_specs=[
            pl.BlockSpec((count, rows_local, GROUP * BLK), lambda g: (0, 0, g)),
            pl.BlockSpec((rows_local, GROUP * BLK), lambda g: (0, g)),
        ],
        out_shape=[
            jax.ShapeDtypeStruct((count, rows_local, side), jnp.float32),
            jax.ShapeDtypeStruct((rows_local, side), jnp.float32),
        ],
        interpret=INTERPRET,
    )(arrived, land_mask, inv_y, vel)


def local(velocity, seed_adjoint, land_mask, inv_x, inv_y, weights):
    con_local = velocity.shape[0]
    cols_local = seed_adjoint.shape[2]
    full_side = seed_adjoint.shape[3]
    rows_local = velocity.shape[2]
    vel_float = velocity.astype(jnp.float32)
    weight_full = weights[:, None, None, None]
    local_squares = jnp.sum(weight_full * vel_float * vel_float, axis=(0, 1))
    sea_float = (land_mask == 1).astype(jnp.float32)
    across = x_solve(seed_adjoint.reshape(con_local * 2 * cols_local, full_side), inv_x)
    arrived = lax.all_to_all(across, "grid", split_axis=0, concat_axis=0, tiled=True)
    arrived, local_squares = lax.optimization_barrier((arrived, local_squares))
    squares = con_sum(local_squares, jnp.bfloat16)
    solved, local_inner = y_solve(arrived, land_mask, inv_y, velocity.reshape(con_local * 2, rows_local, full_side))
    rhs_adjoint = solved.reshape(con_local, 2, rows_local, full_side)
    inner = con_sum(local_inner, jnp.bfloat16)
    speed = jnp.sqrt(0.25 + squares)
    first = -0.5 * sea_float * speed * rhs_adjoint
    second = -0.5 * sea_float * weight_full * vel_float * inner / speed
    return first + second


def solution(mesh):
    return jax.shard_map(
        local,
        mesh=mesh,
        in_specs=(
            P("con", None, "grid", None),
            P("con", None, "grid", None),
            P("grid", None),
            P(),
            P(),
            P("con"),
        ),
        out_specs=P("con", None, "grid", None),
        check_vma=False,
    )
```

```python
import jax
import jax.numpy as jnp
from jax import lax
from jax.experimental import pallas as pl
from jax.experimental.pallas import tpu as pltpu
from jax.sharding import PartitionSpec as P

BLK = 128
GROUP = 16
INTERPRET = False


def con_sum(part, link_type):
    count = lax.axis_size("con")
    me = lax.axis_index("con")
    rows = part.shape[0]
    quarters = part.reshape((count, rows // count) + part.shape[1:])
    total = lax.dynamic_index_in_dim(quarters, me, 0, keepdims=False).astype(jnp.float32)
    for shift in (2, 1, 3):
        pairs = [(i, (i + shift) % count) for i in range(count)]
        piece = lax.dynamic_index_in_dim(quarters, (me + shift) % count, 0, keepdims=False)
        total = total + lax.ppermute(piece.astype(link_type), "con", pairs).astype(jnp.float32)
    mine = total.astype(link_type)
    pieces = {0: mine}
    for shift in (2, 1, 3):
        pairs = [(i, (i + shift) % count) for i in range(count)]
        pieces[shift] = lax.ppermute(mine, "con", pairs)
    slots = []
    for q in range(count):
        source = (me - q) % count
        slot = pieces[0]
        for shift in range(1, count):
            slot = jnp.where(source == shift, pieces[shift], slot)
        slots.append(slot)
    return jnp.concatenate(slots, axis=0).astype(jnp.float32)


def x_solve_kernel(s_ref, w_ref, o_ref):
    for b in range(w_ref.shape[0]):
        block = s_ref[:, b * BLK:(b + 1) * BLK]
        out = lax.dot_general(w_ref[b], block, (((1,), (1,)), ((), ())), preferred_element_type=jnp.float32)
        o_ref[b * BLK:(b + 1) * BLK, :] = out.astype(o_ref.dtype)


def x_solve(rows, inv_x):
    lanes, side = rows.shape
    nblocks = inv_x.shape[0]
    return pl.pallas_call(
        x_solve_kernel,
        grid=(nblocks // GROUP,),
        in_specs=[
            pl.BlockSpec((lanes, GROUP * BLK), lambda g: (0, g)),
            pl.BlockSpec((GROUP, BLK, BLK), lambda g: (g, 0, 0)),
        ],
        out_specs=pl.BlockSpec((GROUP * BLK, lanes), lambda g: (g, 0)),
        out_shape=jax.ShapeDtypeStruct((side, lanes), jnp.bfloat16),
        interpret=INTERPRET,
    )(rows, inv_x)


def y_solve_kernel(r_ref, m_ref, w_ref, v_ref, g_ref, i_ref):
    half = r_ref.shape[0] // (2 * w_ref.shape[0])
    count = v_ref.shape[0]
    lane = lax.broadcasted_iota(jnp.int32, (half, BLK), 1)
    low = lane < half
    for b in range(w_ref.shape[0]):
        cols = slice(b * BLK, (b + 1) * BLK)
        sea = m_ref[:, cols] == 1
        weight = w_ref[b]
        total = jnp.zeros((half, BLK), jnp.float32)
        for q in range(count):
            tile = slice((q // 2) * BLK, (q // 2 + 1) * BLK)
            first = r_ref[2 * b * half:(2 * b + 1) * half, tile]
            second = r_ref[(2 * b + 1) * half:(2 * b + 2) * half, tile]
            if q % 2 == 0:
                joined = jnp.where(low, first, pltpu.roll(second, half, 1))
            else:
                joined = jnp.where(low, pltpu.roll(first, half, 1), second)
            joined = jnp.where(sea, joined, jnp.zeros_like(joined))
            out = lax.dot_general(joined, weight, (((1,), (1,)), ((), ())), preferred_element_type=jnp.float32)
            g_ref[q, :, cols] = out
            total = total + out * v_ref[q, :, cols].astype(jnp.float32)
        i_ref[:, cols] = total.astype(i_ref.dtype)


def y_solve(arrived, land_mask, inv_y, vel):
    count, rows_local, side = vel.shape
    nblocks = inv_y.shape[0]
    return pl.pallas_call(
        y_solve_kernel,
        grid=(nblocks // GROUP,),
        in_specs=[
            pl.BlockSpec((GROUP * 2 * rows_local, arrived.shape[1]), lambda g: (g, 0)),
            pl.BlockSpec((rows_local, GROUP * BLK), lambda g: (0, g)),
            pl.BlockSpec((GROUP, BLK, BLK), lambda g: (g, 0, 0)),
            pl.BlockSpec((count, rows_local, GROUP * BLK), lambda g: (0, 0, g)),
        ],
        out_specs=[
            pl.BlockSpec((count, rows_local, GROUP * BLK), lambda g: (0, 0, g)),
            pl.BlockSpec((rows_local, GROUP * BLK), lambda g: (0, g)),
        ],
        out_shape=[
            jax.ShapeDtypeStruct((count, rows_local, side), jnp.float32),
            jax.ShapeDtypeStruct((rows_local, side), jnp.bfloat16),
        ],
        interpret=INTERPRET,
    )(arrived, land_mask, inv_y, vel)


def local(velocity, seed_adjoint, land_mask, inv_x, inv_y, weights):
    con_local = velocity.shape[0]
    cols_local = seed_adjoint.shape[2]
    full_side = seed_adjoint.shape[3]
    rows_local = velocity.shape[2]
    vel_float = velocity.astype(jnp.float32)
    weight_full = weights[:, None, None, None]
    local_squares = jnp.sum(weight_full * vel_float * vel_float, axis=(0, 1))
    sea_float = (land_mask == 1).astype(jnp.float32)
    across = x_solve(seed_adjoint.reshape(con_local * 2 * cols_local, full_side), inv_x)
    arrived = lax.all_to_all(across, "grid", split_axis=0, concat_axis=0, tiled=True)
    arrived, local_squares = lax.optimization_barrier((arrived, local_squares))
    squares = con_sum(local_squares, jnp.bfloat16)
    solved, local_inner = y_solve(arrived, land_mask, inv_y, velocity.reshape(con_local * 2, rows_local, full_side))
    rhs_adjoint = solved.reshape(con_local, 2, rows_local, full_side)
    inner = con_sum(local_inner, jnp.bfloat16)
    speed = jnp.sqrt(0.25 + squares)
    first = -0.5 * sea_float * speed * rhs_adjoint
    second = -0.5 * sea_float * weight_full * vel_float * inner / speed
    return first + second


def solution(mesh):
    return jax.shard_map(
        local,
        mesh=mesh,
        in_specs=(
            P("con", None, "grid", None),
            P("con", None, "grid", None),
            P("grid", None),
            P(),
            P(),
            P("con"),
        ),
        out_specs=P("con", None, "grid", None),
        check_vma=False,
    )
```

```python
import jax
import jax.numpy as jnp
from jax import lax
from jax.experimental import pallas as pl
from jax.experimental.pallas import tpu as pltpu
from jax.sharding import PartitionSpec as P

BLK = 128
GROUP = 16
INTERPRET = False


def con_sum(part, link_type):
    count = lax.axis_size("con")
    me = lax.axis_index("con")
    rows = part.shape[0]
    quarters = part.reshape((count, rows // count) + part.shape[1:])
    total = lax.dynamic_index_in_dim(quarters, me, 0, keepdims=False).astype(jnp.float32)
    for shift in (2, 1, 3):
        pairs = [(i, (i + shift) % count) for i in range(count)]
        piece = lax.dynamic_index_in_dim(quarters, (me + shift) % count, 0, keepdims=False)
        total = total + lax.ppermute(piece.astype(link_type), "con", pairs).astype(jnp.float32)
    mine = total.astype(link_type)
    pieces = {0: mine}
    for shift in (2, 1, 3):
        pairs = [(i, (i + shift) % count) for i in range(count)]
        pieces[shift] = lax.ppermute(mine, "con", pairs)
    slots = []
    for q in range(count):
        source = (me - q) % count
        slot = pieces[0]
        for shift in range(1, count):
            slot = jnp.where(source == shift, pieces[shift], slot)
        slots.append(slot)
    return jnp.concatenate(slots, axis=0).astype(jnp.float32)


def x_solve_kernel(s_ref, w_ref, o_ref):
    for b in range(w_ref.shape[0]):
        block = s_ref[:, b * BLK:(b + 1) * BLK]
        out = lax.dot_general(w_ref[b], block, (((1,), (1,)), ((), ())), preferred_element_type=jnp.float32)
        o_ref[b * BLK:(b + 1) * BLK, :] = out.astype(o_ref.dtype)


def x_solve(rows, inv_x):
    lanes, side = rows.shape
    nblocks = inv_x.shape[0]
    return pl.pallas_call(
        x_solve_kernel,
        grid=(nblocks // GROUP,),
        in_specs=[
            pl.BlockSpec((lanes, GROUP * BLK), lambda g: (0, g)),
            pl.BlockSpec((GROUP, BLK, BLK), lambda g: (g, 0, 0)),
        ],
        out_specs=pl.BlockSpec((GROUP * BLK, lanes), lambda g: (g, 0)),
        out_shape=jax.ShapeDtypeStruct((side, lanes), jnp.bfloat16),
        interpret=INTERPRET,
    )(rows, inv_x)


def y_solve_kernel(r_ref, m_ref, w_ref, v_ref, g_ref, i_ref):
    half = r_ref.shape[0] // (2 * w_ref.shape[0])
    count = v_ref.shape[0]
    lane = lax.broadcasted_iota(jnp.int32, (half, BLK), 1)
    low = lane < half
    for b in range(w_ref.shape[0]):
        cols = slice(b * BLK, (b + 1) * BLK)
        sea = m_ref[:, cols] == 1
        weight = w_ref[b]
        total = jnp.zeros((half, BLK), jnp.float32)
        for q in range(count):
            tile = slice((q // 2) * BLK, (q // 2 + 1) * BLK)
            first = r_ref[2 * b * half:(2 * b + 1) * half, tile]
            second = r_ref[(2 * b + 1) * half:(2 * b + 2) * half, tile]
            if q % 2 == 0:
                joined = jnp.where(low, first, pltpu.roll(second, half, 1))
            else:
                joined = jnp.where(low, pltpu.roll(first, half, 1), second)
            joined = jnp.where(sea, joined, jnp.zeros_like(joined))
            out = lax.dot_general(joined, weight, (((1,), (1,)), ((), ())), preferred_element_type=jnp.float32)
            g_ref[q, :, cols] = out.astype(g_ref.dtype)
            total = total + out * v_ref[q, :, cols].astype(jnp.float32)
        i_ref[:, cols] = total.astype(i_ref.dtype)


def y_solve(arrived, land_mask, inv_y, vel):
    count, rows_local, side = vel.shape
    nblocks = inv_y.shape[0]
    return pl.pallas_call(
        y_solve_kernel,
        grid=(nblocks // GROUP,),
        in_specs=[
            pl.BlockSpec((GROUP * 2 * rows_local, arrived.shape[1]), lambda g: (g, 0)),
            pl.BlockSpec((rows_local, GROUP * BLK), lambda g: (0, g)),
            pl.BlockSpec((GROUP, BLK, BLK), lambda g: (g, 0, 0)),
            pl.BlockSpec((count, rows_local, GROUP * BLK), lambda g: (0, 0, g)),
        ],
        out_specs=[
            pl.BlockSpec((count, rows_local, GROUP * BLK), lambda g: (0, 0, g)),
            pl.BlockSpec((rows_local, GROUP * BLK), lambda g: (0, g)),
        ],
        out_shape=[
            jax.ShapeDtypeStruct((count, rows_local, side), jnp.bfloat16),
            jax.ShapeDtypeStruct((rows_local, side), jnp.bfloat16),
        ],
        interpret=INTERPRET,
    )(arrived, land_mask, inv_y, vel)


def local(velocity, seed_adjoint, land_mask, inv_x, inv_y, weights):
    con_local = velocity.shape[0]
    cols_local = seed_adjoint.shape[2]
    full_side = seed_adjoint.shape[3]
    rows_local = velocity.shape[2]
    vel_float = velocity.astype(jnp.float32)
    weight_full = weights[:, None, None, None]
    local_squares = jnp.sum(weight_full * vel_float * vel_float, axis=(0, 1))
    sea_float = (land_mask == 1).astype(jnp.float32)
    across = x_solve(seed_adjoint.reshape(con_local * 2 * cols_local, full_side), inv_x)
    arrived = lax.all_to_all(across, "grid", split_axis=0, concat_axis=0, tiled=True)
    arrived, local_squares = lax.optimization_barrier((arrived, local_squares))
    squares = con_sum(local_squares, jnp.bfloat16)
    solved, local_inner = y_solve(arrived, land_mask, inv_y, velocity.reshape(con_local * 2, rows_local, full_side))
    rhs_adjoint = solved.reshape(con_local, 2, rows_local, full_side)
    inner = con_sum(local_inner, jnp.bfloat16)
    speed = jnp.sqrt(0.25 + squares)
    first = -0.5 * sea_float * speed * rhs_adjoint
    second = -0.5 * sea_float * weight_full * vel_float * inner / speed
    return first + second


def solution(mesh):
    return jax.shard_map(
        local,
        mesh=mesh,
        in_specs=(
            P("con", None, "grid", None),
            P("con", None, "grid", None),
            P("grid", None),
            P(),
            P(),
            P("con"),
        ),
        out_specs=P("con", None, "grid", None),
        check_vma=False,
    )
```

```python
import jax
import jax.numpy as jnp
from jax import lax
from jax.experimental import pallas as pl
from jax.experimental.pallas import tpu as pltpu
from jax.sharding import PartitionSpec as P

BLK = 128
GROUP = 16
Y_GROUP = 8
INTERPRET = False


def con_sum(part, link_type):
    count = lax.axis_size("con")
    me = lax.axis_index("con")
    rows = part.shape[0]
    quarters = part.reshape((count, rows // count) + part.shape[1:])
    total = lax.dynamic_index_in_dim(quarters, me, 0, keepdims=False).astype(jnp.float32)
    for shift in (2, 1, 3):
        pairs = [(i, (i + shift) % count) for i in range(count)]
        piece = lax.dynamic_index_in_dim(quarters, (me + shift) % count, 0, keepdims=False)
        total = total + lax.ppermute(piece.astype(link_type), "con", pairs).astype(jnp.float32)
    mine = total.astype(link_type)
    pieces = {0: mine}
    for shift in (2, 1, 3):
        pairs = [(i, (i + shift) % count) for i in range(count)]
        pieces[shift] = lax.ppermute(mine, "con", pairs)
    slots = []
    for q in range(count):
        source = (me - q) % count
        slot = pieces[0]
        for shift in range(1, count):
            slot = jnp.where(source == shift, pieces[shift], slot)
        slots.append(slot)
    return jnp.concatenate(slots, axis=0).astype(jnp.float32)


def x_solve_kernel(s_ref, w_ref, o_ref):
    for b in range(w_ref.shape[0]):
        block = s_ref[:, b * BLK:(b + 1) * BLK]
        out = lax.dot_general(w_ref[b], block, (((1,), (1,)), ((), ())), preferred_element_type=jnp.float32)
        o_ref[b * BLK:(b + 1) * BLK, :] = out.astype(o_ref.dtype)


def x_solve(rows, inv_x):
    lanes, side = rows.shape
    nblocks = inv_x.shape[0]
    return pl.pallas_call(
        x_solve_kernel,
        grid=(nblocks // GROUP,),
        in_specs=[
            pl.BlockSpec((lanes, GROUP * BLK), lambda g: (0, g)),
            pl.BlockSpec((GROUP, BLK, BLK), lambda g: (g, 0, 0)),
        ],
        out_specs=pl.BlockSpec((GROUP * BLK, lanes), lambda g: (g, 0)),
        out_shape=jax.ShapeDtypeStruct((side, lanes), jnp.bfloat16),
        interpret=INTERPRET,
    )(rows, inv_x)


def y_solve_kernel(r_ref, m_ref, w_ref, v_ref, g_ref, i_ref):
    half = r_ref.shape[0] // (2 * w_ref.shape[0])
    count = v_ref.shape[0]
    lane = lax.broadcasted_iota(jnp.int32, (half, BLK), 1)
    low = lane < half
    for b in range(w_ref.shape[0]):
        cols = slice(b * BLK, (b + 1) * BLK)
        sea = m_ref[:, cols] == 1
        weight = w_ref[b]
        total = jnp.zeros((half, BLK), jnp.float32)
        for q in range(count):
            tile = slice((q // 2) * BLK, (q // 2 + 1) * BLK)
            first = r_ref[2 * b * half:(2 * b + 1) * half, tile]
            second = r_ref[(2 * b + 1) * half:(2 * b + 2) * half, tile]
            if q % 2 == 0:
                joined = jnp.where(low, first, pltpu.roll(second, half, 1))
            else:
                joined = jnp.where(low, pltpu.roll(first, half, 1), second)
            joined = jnp.where(sea, joined, jnp.zeros_like(joined))
            out = lax.dot_general(joined, weight, (((1,), (1,)), ((), ())), preferred_element_type=jnp.float32)
            g_ref[q, :, cols] = out
            total = total + out * v_ref[q, :, cols].astype(jnp.float32)
        i_ref[:, cols] = total.astype(i_ref.dtype)


def y_solve(arrived, land_mask, inv_y, vel):
    count, rows_local, side = vel.shape
    nblocks = inv_y.shape[0]
    return pl.pallas_call(
        y_solve_kernel,
        grid=(nblocks // Y_GROUP,),
        in_specs=[
            pl.BlockSpec((Y_GROUP * 2 * rows_local, arrived.shape[1]), lambda g: (g, 0)),
            pl.BlockSpec((rows_local, Y_GROUP * BLK), lambda g: (0, g)),
            pl.BlockSpec((Y_GROUP, BLK, BLK), lambda g: (g, 0, 0)),
            pl.BlockSpec((count, rows_local, Y_GROUP * BLK), lambda g: (0, 0, g)),
        ],
        out_specs=[
            pl.BlockSpec((count, rows_local, Y_GROUP * BLK), lambda g: (0, 0, g)),
            pl.BlockSpec((rows_local, Y_GROUP * BLK), lambda g: (0, g)),
        ],
        out_shape=[
            jax.ShapeDtypeStruct((count, rows_local, side), jnp.float32),
            jax.ShapeDtypeStruct((rows_local, side), jnp.bfloat16),
        ],
        interpret=INTERPRET,
    )(arrived, land_mask, inv_y, vel)


def local(velocity, seed_adjoint, land_mask, inv_x, inv_y, weights):
    con_local = velocity.shape[0]
    cols_local = seed_adjoint.shape[2]
    full_side = seed_adjoint.shape[3]
    rows_local = velocity.shape[2]
    vel_float = velocity.astype(jnp.float32)
    weight_full = weights[:, None, None, None]
    local_squares = jnp.sum(weight_full * vel_float * vel_float, axis=(0, 1))
    sea_float = (land_mask == 1).astype(jnp.float32)
    across = x_solve(seed_adjoint.reshape(con_local * 2 * cols_local, full_side), inv_x)
    arrived = lax.all_to_all(across, "grid", split_axis=0, concat_axis=0, tiled=True)
    arrived, local_squares = lax.optimization_barrier((arrived, local_squares))
    squares = con_sum(local_squares, jnp.bfloat16)
    solved, local_inner = y_solve(arrived, land_mask, inv_y, velocity.reshape(con_local * 2, rows_local, full_side))
    rhs_adjoint = solved.reshape(con_local, 2, rows_local, full_side)
    inner = con_sum(local_inner, jnp.bfloat16)
    speed = jnp.sqrt(0.25 + squares)
    first = -0.5 * sea_float * speed * rhs_adjoint
    second = -0.5 * sea_float * weight_full * vel_float * inner / speed
    return first + second


def solution(mesh):
    return jax.shard_map(
        local,
        mesh=mesh,
        in_specs=(
            P("con", None, "grid", None),
            P("con", None, "grid", None),
            P("grid", None),
            P(),
            P(),
            P("con"),
        ),
        out_specs=P("con", None, "grid", None),
        check_vma=False,
    )
```

```python
import jax
import jax.numpy as jnp
from jax import lax
from jax.experimental import pallas as pl
from jax.experimental.pallas import tpu as pltpu
from jax.sharding import PartitionSpec as P

BLK = 128
GROUP = 16
X_GROUP = 32
INTERPRET = False


def con_sum(part, link_type):
    count = lax.axis_size("con")
    me = lax.axis_index("con")
    rows = part.shape[0]
    quarters = part.reshape((count, rows // count) + part.shape[1:])
    total = lax.dynamic_index_in_dim(quarters, me, 0, keepdims=False).astype(jnp.float32)
    for shift in (2, 1, 3):
        pairs = [(i, (i + shift) % count) for i in range(count)]
        piece = lax.dynamic_index_in_dim(quarters, (me + shift) % count, 0, keepdims=False)
        total = total + lax.ppermute(piece.astype(link_type), "con", pairs).astype(jnp.float32)
    mine = total.astype(link_type)
    pieces = {0: mine}
    for shift in (2, 1, 3):
        pairs = [(i, (i + shift) % count) for i in range(count)]
        pieces[shift] = lax.ppermute(mine, "con", pairs)
    slots = []
    for q in range(count):
        source = (me - q) % count
        slot = pieces[0]
        for shift in range(1, count):
            slot = jnp.where(source == shift, pieces[shift], slot)
        slots.append(slot)
    return jnp.concatenate(slots, axis=0).astype(jnp.float32)


def x_solve_kernel(s_ref, w_ref, o_ref):
    for b in range(w_ref.shape[0]):
        block = s_ref[:, b * BLK:(b + 1) * BLK]
        out = lax.dot_general(w_ref[b], block, (((1,), (1,)), ((), ())), preferred_element_type=jnp.float32)
        o_ref[b * BLK:(b + 1) * BLK, :] = out.astype(o_ref.dtype)


def x_solve(rows, inv_x):
    lanes, side = rows.shape
    nblocks = inv_x.shape[0]
    return pl.pallas_call(
        x_solve_kernel,
        grid=(nblocks // X_GROUP,),
        in_specs=[
            pl.BlockSpec((lanes, X_GROUP * BLK), lambda g: (0, g)),
            pl.BlockSpec((X_GROUP, BLK, BLK), lambda g: (g, 0, 0)),
        ],
        out_specs=pl.BlockSpec((X_GROUP * BLK, lanes), lambda g: (g, 0)),
        out_shape=jax.ShapeDtypeStruct((side, lanes), jnp.bfloat16),
        interpret=INTERPRET,
    )(rows, inv_x)


def y_solve_kernel(r_ref, m_ref, w_ref, v_ref, g_ref, i_ref):
    half = r_ref.shape[0] // (2 * w_ref.shape[0])
    count = v_ref.shape[0]
    lane = lax.broadcasted_iota(jnp.int32, (half, BLK), 1)
    low = lane < half
    for b in range(w_ref.shape[0]):
        cols = slice(b * BLK, (b + 1) * BLK)
        sea = m_ref[:, cols] == 1
        weight = w_ref[b]
        total = jnp.zeros((half, BLK), jnp.float32)
        for q in range(count):
            tile = slice((q // 2) * BLK, (q // 2 + 1) * BLK)
            first = r_ref[2 * b * half:(2 * b + 1) * half, tile]
            second = r_ref[(2 * b + 1) * half:(2 * b + 2) * half, tile]
            if q % 2 == 0:
                joined = jnp.where(low, first, pltpu.roll(second, half, 1))
            else:
                joined = jnp.where(low, pltpu.roll(first, half, 1), second)
            joined = jnp.where(sea, joined, jnp.zeros_like(joined))
            out = lax.dot_general(joined, weight, (((1,), (1,)), ((), ())), preferred_element_type=jnp.float32)
            g_ref[q, :, cols] = out
            total = total + out * v_ref[q, :, cols].astype(jnp.float32)
        i_ref[:, cols] = total.astype(i_ref.dtype)


def y_solve(arrived, land_mask, inv_y, vel):
    count, rows_local, side = vel.shape
    nblocks = inv_y.shape[0]
    return pl.pallas_call(
        y_solve_kernel,
        grid=(nblocks // GROUP,),
        in_specs=[
            pl.BlockSpec((GROUP * 2 * rows_local, arrived.shape[1]), lambda g: (g, 0)),
            pl.BlockSpec((rows_local, GROUP * BLK), lambda g: (0, g)),
            pl.BlockSpec((GROUP, BLK, BLK), lambda g: (g, 0, 0)),
            pl.BlockSpec((count, rows_local, GROUP * BLK), lambda g: (0, 0, g)),
        ],
        out_specs=[
            pl.BlockSpec((count, rows_local, GROUP * BLK), lambda g: (0, 0, g)),
            pl.BlockSpec((rows_local, GROUP * BLK), lambda g: (0, g)),
        ],
        out_shape=[
            jax.ShapeDtypeStruct((count, rows_local, side), jnp.float32),
            jax.ShapeDtypeStruct((rows_local, side), jnp.bfloat16),
        ],
        interpret=INTERPRET,
    )(arrived, land_mask, inv_y, vel)


def local(velocity, seed_adjoint, land_mask, inv_x, inv_y, weights):
    con_local = velocity.shape[0]
    cols_local = seed_adjoint.shape[2]
    full_side = seed_adjoint.shape[3]
    rows_local = velocity.shape[2]
    vel_float = velocity.astype(jnp.float32)
    weight_full = weights[:, None, None, None]
    local_squares = jnp.sum(weight_full * vel_float * vel_float, axis=(0, 1))
    sea_float = (land_mask == 1).astype(jnp.float32)
    across = x_solve(seed_adjoint.reshape(con_local * 2 * cols_local, full_side), inv_x)
    arrived = lax.all_to_all(across, "grid", split_axis=0, concat_axis=0, tiled=True)
    arrived, local_squares = lax.optimization_barrier((arrived, local_squares))
    squares = con_sum(local_squares, jnp.bfloat16)
    solved, local_inner = y_solve(arrived, land_mask, inv_y, velocity.reshape(con_local * 2, rows_local, full_side))
    rhs_adjoint = solved.reshape(con_local, 2, rows_local, full_side)
    inner = con_sum(local_inner, jnp.bfloat16)
    speed = jnp.sqrt(0.25 + squares)
    first = -0.5 * sea_float * speed * rhs_adjoint
    second = -0.5 * sea_float * weight_full * vel_float * inner / speed
    return first + second


def solution(mesh):
    return jax.shard_map(
        local,
        mesh=mesh,
        in_specs=(
            P("con", None, "grid", None),
            P("con", None, "grid", None),
            P("grid", None),
            P(),
            P(),
            P("con"),
        ),
        out_specs=P("con", None, "grid", None),
        check_vma=False,
    )
```
